128 devices in a mesh: req: 32 (over y, x, core), head: 4 (over z).
Axes of the slice: x: 4, y: 4, z: 4, core: 2. Of those that a mesh axis runs over, the one named last changes fastest.
Arguments:
- tokens: bfloat16 [2048, 2048], P(('req', 'head')), may hold values from -6 to 6
- attn_gain: bfloat16 [2048], replicated, may hold values from 0.099609375 to 1.8984375
- w_query: bfloat16 [2048, 2048], P(None, 'head'), may hold values from -0.125 to 0.125
- w_key: bfloat16 [2048, 512], P(None, 'head'), may hold values from -0.125 to 0.125
- w_value: bfloat16 [2048, 512], P(None, 'head'), may hold values from -0.125 to 0.125
- w_out: bfloat16 [2048, 2048], P('head'), may hold values from -0.5 to 0.5
- key_cache: bfloat16 [778240, 512], P('req', 'head'), may hold values from -305 to 305
- value_cache: bfloat16 [778240, 512], P('req', 'head'), may hold values from -6 to 6
- lengths: int32 [2048], P('req'), may hold values from 64 to 8192, as said below
- ffn_gain: bfloat16 [2048], replicated, may hold values from 0.099609375 to 1.8984375
- shared_gate: bfloat16 [2048, 1408], P(None, 'head'), may hold values from -0.125 to 0.125
- shared_up: bfloat16 [2048, 1408], P(None, 'head'), may hold values from -0.125 to 0.125
- shared_down: bfloat16 [1408, 2048], P('head'), may hold values from -0.15625 to 0.15625
- expert_gate: bfloat16 [128, 2048, 704], P(('req', 'head')), may hold values from -0.125 to 0.125
- expert_up: bfloat16 [128, 2048, 704], P(('req', 'head')), may hold values from -0.125 to 0.125
- expert_down: bfloat16 [128, 704, 2048], P(('req', 'head')), may hold values from -0.15625 to 0.15625
- route_idx: int32 [2048, 6], P(('req', 'head')), may hold values from 0 to 63, all different within a row; in each aligned block of 16 rows (0 to 15, 16 to 31, ...) at most 2 rows name the same one
- route_wt: float32 [2048, 6], P(('req', 'head')), may hold values from 0.2 to 2
Outputs:
- result: bfloat16 [2048, 2048], P(('req', 'head'))
- new_kv: bfloat16 [2, 2048, 512], P(None, 'req', 'head')
The draws below stay inside these ranges and needn't reach their ends.
Inputs may be any that keep to these rules, and one draw needn't show every extreme that they name: Exactly two requests have length 8192, in different blocks of 64 requests; all others have lengths from 64 to 256. `route_idx`: among the 16 tokens of one device (aligned blocks of rows) no expert is picked more than 2 times; a token's picks differ.
All inputs are finite; a program needn't handle non-finite values.
Results may differ from the reference program's by a relative error of at most 0.019.
The reference program's roundings to bfloat16 on the way count: a program that leaves them out, or rounds other values in their place, can miss the bound.
Values may be sent and summed in bfloat16 or wider, within the bound.
No kernel may reach another device: no remote copies, remote signals or barrier semaphores. Data moves between devices by JAX's collectives and lax.ppermute only.
A program may use at most 128 MiB of HBM per device.

```python
import math
import jax
import jax.numpy as jnp
import numpy as np
from jax import lax

D = 2048
QH = 16
KVH = 4
HD = 128
FF = 1408
SFF = 1408
TOPK = 6
RPD = 64
LONG = 8192
SHORT_MIN = 64
SHORT_MAX = 256
E = 64
REQS = 2048
TOK_DEV = 16
CAP = 24320
MOST = 2
N_REQ = 32


def draw_tokens(key, part):
    subkeys = jax.random.split(jax.random.fold_in(key, 11), 3)
    row_scale = jnp.exp(jax.random.uniform(subkeys[0], (REQS, 1), jnp.float32, math.log(0.1), math.log(1.0)))
    col_scale = jnp.exp(jax.random.uniform(subkeys[1], (1, D), jnp.float32, math.log(0.5), math.log(2.0)))
    base = jnp.clip(jax.random.normal(subkeys[2], (REQS, D), jnp.float32), -3.0, 3.0)
    return (base * row_scale * col_scale).astype(jnp.bfloat16)


def draw_key_cache(key, part):
    total_rows = REQS // RPD * CAP
    subkeys = jax.random.split(jax.random.fold_in(key, 23), 1)
    base = jnp.clip(jax.random.normal(subkeys[0], (total_rows, KVH * HD), jnp.float32), -3.0, 3.0)
    return base.astype(jnp.bfloat16)


def draw_lengths(key, part):
    blocks_total = REQS // RPD
    subkeys = jax.random.split(jax.random.fold_in(key, 37), 3)
    short_rows = jax.random.randint(subkeys[0], (REQS,), SHORT_MIN, SHORT_MAX + 1, dtype=jnp.int32)
    chosen_blocks = jax.random.permutation(subkeys[1], blocks_total)[:2].astype(jnp.int32)
    offsets = jax.random.randint(subkeys[2], (2,), 0, RPD, dtype=jnp.int32)
    long_rows = chosen_blocks * RPD + offsets
    return short_rows.at[long_rows].set(LONG)


def steps_of(stream_key, dims, pieces, smallest, largest):
    factor_of = 1.0
    for axis_at, blocks in pieces:
        draws = jax.random.uniform(jax.random.fold_in(jax.random.fold_in(stream_key, 6), axis_at), (blocks,), jnp.float32, smallest / len(pieces), largest / len(pieces))
        factor_of = factor_of * jnp.repeat(jnp.exp(draws), dims[axis_at] // blocks).reshape((-1,) + (1,) * (len(dims) - 1 - axis_at))
    return factor_of


def shared_out(own_key, own, number, rows, number_of, top, bound, lean):
    sequence = jax.random.permutation(own_key, number_of)
    packed, common = shares(number_of, rows * top, bound, lean, True), shares(number_of, rows * top, bound, lean, False)
    places = jnp.arange(number_of)

    def named(tallies, turn):
        used = int((tallies > 0).sum())
        fixed = max(1, used // 4)
        moved = fixed + (places - fixed + turn * (used - fixed)) % max(1, number_of - fixed)
        return jnp.zeros((number_of,), jnp.int32).at[sequence[jnp.where(places < fixed, places, moved)]].set(jnp.asarray(tallies, jnp.int32))

    tallies = jnp.where(number % 4 == 0, named(packed, number // 4), named(common, number - number // 4 - 1))
    mixed = jax.random.permutation(jax.random.fold_in(own, 3), number_of)
    donor, sink = mixed[0:number_of // 2 * 2:2], mixed[1:number_of // 2 * 2:2]
    margin = jnp.minimum(tallies[donor] - 1, bound - tallies[sink]) // 2
    margin = jnp.where((donor == sequence[0]) | (sink == sequence[0]) | (tallies[sink] == 0), 0, jnp.maximum(margin, 0))
    moved = jax.random.randint(jax.random.fold_in(own, 4), (number_of // 2,), 0, 1 << 20) % (margin + 1)
    tallies = tallies.at[donor].add(-moved).at[sink].add(moved)
    members = jnp.searchsorted(jnp.cumsum(tallies), jnp.arange(rows * top), side="right").astype(jnp.int32)
    table = members.reshape(top, rows).T
    table = table[jax.random.permutation(jax.random.fold_in(own, 1), rows)]
    turn = jax.random.randint(jax.random.fold_in(own, 2), (rows, 1), 0, top)
    return jnp.take_along_axis(table, (jnp.arange(top)[None, :] + turn) % top, axis=1)


def shares(amount, total, bound, lean, full):
    portions = [(1 << 20) // math.isqrt(rank ** lean) + 1 for rank in range(1, amount + 1)]
    largest = bound if full else min(bound, max(-(-total // amount), total * portions[0] // sum(portions)))
    least = 1 if total - largest >= amount - 1 else 0
    given, rest = [largest] + [least] * (amount - 1), total - largest - least * (amount - 1)
    while rest > 0:
        movable = [i for i in range(1, amount) if given[i] < largest] or [i for i in range(1, amount) if given[i] < bound]
        mass, budget = sum([portions[i] for i in movable]), rest
        for i in movable:
            more = min(bound - given[i], max(1, budget * portions[i] // mass), rest)
            given[i] = given[i] + more
            rest = rest - more
    return np.array(given)


def centred(rng, extent, width, reach, shards=(), held_as=jnp.bfloat16):
    level = steps_of(rng, extent, shards, -0.22, 0.18) if shards else 1.0
    array = jax.random.normal(rng, extent, jnp.float32) * width * level
    return jnp.minimum(jnp.maximum(array, -reach), reach).astype(held_as)


def setup_inputs(seed: int = 0) -> dict:
    key_list = jax.random.split(jax.random.key(seed), 19)
    tokens = draw_tokens(jax.random.fold_in(key_list[18], 71), 0)
    attn_gain = jnp.clip(1.0 + 0.18 * jax.random.normal(key_list[1], (D,), jnp.float32), 0.099609375, 1.8984375).astype(jnp.bfloat16)
    w_query = centred(key_list[2], (D, QH * HD), D ** -0.5, 0.125, ((1, 4),))
    w_key = centred(key_list[3], (D, KVH * HD), D ** -0.5, 0.125, ((1, 4),))
    w_value = centred(key_list[4], (D, KVH * HD), D ** -0.5, 0.125, ((1, 4),))
    w_out = centred(key_list[5], (QH * HD, D), HD ** -0.5, 0.5, ((0, 4),))
    key_cache = draw_key_cache(jax.random.fold_in(key_list[18], 71), 0)
    value_cache = centred(key_list[7], (N_REQ * CAP, KVH * HD), 1.0, 6.0, ((0, 32), (1, 4)))
    lengths = draw_lengths(jax.random.fold_in(key_list[18], 71), 0)
    ffn_gain = jnp.clip(1.0 + 0.18 * jax.random.normal(key_list[9], (D,), jnp.float32), 0.099609375, 1.8984375).astype(jnp.bfloat16)
    shared_gate = centred(key_list[10], (D, SFF), D ** -0.5, 0.125, ((1, 4),))
    shared_up = centred(key_list[11], (D, SFF), D ** -0.5, 0.125, ((1, 4),))
    shared_down = centred(key_list[12], (SFF, D), SFF ** -0.5, 0.15625, ((0, 4),))
    expert_gate = centred(key_list[13], (2 * E, D, FF // 2), D ** -0.5, 0.125, ((0, 128),))
    expert_up = centred(key_list[14], (2 * E, D, FF // 2), D ** -0.5, 0.125, ((0, 128),))
    expert_down = centred(key_list[15], (2 * E, FF // 2, D), FF ** -0.5, 0.15625, ((0, 128),))
    route_idx_keys = jax.random.split(jax.random.fold_in(key_list[16], 1), REQS // TOK_DEV)
    route_idx_turns = jax.random.permutation(jax.random.fold_in(key_list[16], 3), REQS // TOK_DEV)
    route_idx = jax.vmap(lambda own, number: shared_out(jax.random.fold_in(key_list[16], 2), own, number, TOK_DEV, E, TOPK, MOST, 2))(route_idx_keys, route_idx_turns).reshape((REQS, TOPK))
    route_wt = jnp.clip(jnp.exp(math.log(2.0) - 2.3025851 * jax.random.uniform(key_list[17], (REQS, TOPK), jnp.float32) ** steps_of(key_list[17], (REQS, TOPK), ((0, 128),), -0.2, 0.2)), 0.2, 2.0)
    return {"tokens": tokens, "attn_gain": attn_gain, "w_query": w_query, "w_key": w_key, "w_value": w_value, "w_out": w_out, "key_cache": key_cache, "value_cache": value_cache, "lengths": lengths, "ffn_gain": ffn_gain, "shared_gate": shared_gate, "shared_up": shared_up, "shared_down": shared_down, "expert_gate": expert_gate, "expert_up": expert_up, "expert_down": expert_down, "route_idx": route_idx, "route_wt": route_wt}


EPS = 1e-06
ROPE_BASE = 10000.0

def rms_scale(row_data, gain):
    widened = row_data.astype(jnp.float32)
    return widened * lax.rsqrt(lax.optimization_barrier(jnp.mean(widened * widened, axis=-1, keepdims=True)) + EPS) * gain.astype(jnp.float32)

def rotate(vectors, positions):
    half_dim = vectors.shape[-1] // 2
    steps_idx = jnp.arange(half_dim, dtype=jnp.float32)
    frequency = jnp.exp(-(2.0 * steps_idx / vectors.shape[-1]) * math.log(ROPE_BASE))
    angles = positions.astype(jnp.float32)[:, None] * frequency[None, :]
    cosine = jnp.cos(angles)[:, None, :]
    sine_part = jnp.sin(angles)[:, None, :]
    first_half = vectors[..., :half_dim]
    second_half = vectors[..., half_dim:]
    return jnp.concatenate([first_half * cosine - second_half * sine_part, second_half * cosine + first_half * sine_part], axis=-1)

def swiglu_rows(row_data, w_gate, w_up):
    gate_part = jnp.dot(row_data, w_gate, preferred_element_type=jnp.float32)
    up_part = jnp.dot(row_data, w_up, preferred_element_type=jnp.float32)
    return (jax.nn.silu(gate_part) * up_part).astype(jnp.bfloat16)

def reference(tokens, attn_gain, w_query, w_key, w_value, w_out, key_cache, value_cache, lengths, ffn_gain, shared_gate, shared_up, shared_down, expert_gate, expert_up, expert_down, route_idx, route_wt):
    group_size = QH // KVH
    normed = rms_scale(tokens, attn_gain).astype(jnp.bfloat16)
    queries = rotate(jnp.dot(normed, w_query, preferred_element_type=jnp.float32).reshape(REQS, QH, HD), lengths).astype(jnp.bfloat16)
    new_key = rotate(jnp.dot(normed, w_key, preferred_element_type=jnp.float32).reshape(REQS, KVH, HD), lengths).astype(jnp.bfloat16)
    new_value = jnp.dot(normed, w_value, preferred_element_type=jnp.float32).astype(jnp.bfloat16).reshape(REQS, KVH, HD)
    score_scale = 1.0 / math.sqrt(HD)
    blocks_total = REQS // RPD

    def attend(block_index):
        query_f = lax.dynamic_slice_in_dim(queries, block_index * RPD, RPD, 0).astype(jnp.float32).reshape(RPD, KVH, group_size, HD)
        fresh_key = lax.dynamic_slice_in_dim(new_key, block_index * RPD, RPD, 0).astype(jnp.float32)
        fresh_value = lax.dynamic_slice_in_dim(new_value, block_index * RPD, RPD, 0).astype(jnp.float32)
        cache_keys = lax.dynamic_slice_in_dim(key_cache, block_index * CAP, CAP, 0).astype(jnp.float32).reshape(CAP, KVH, HD)
        cache_values = lax.dynamic_slice_in_dim(value_cache, block_index * CAP, CAP, 0).astype(jnp.float32).reshape(CAP, KVH, HD)
        block_lengths = lax.dynamic_slice_in_dim(lengths, block_index * RPD, RPD, 0)
        starts = jnp.cumsum(block_lengths) - block_lengths
        row_ids = jnp.arange(CAP, dtype=jnp.int32)
        visible = (row_ids[None, :] >= starts[:, None]) & (row_ids[None, :] < (starts + block_lengths)[:, None])
        scores = jnp.einsum('rkgd,ckd->rkgc', query_f, cache_keys) * score_scale
        own_score = jnp.einsum('rkgd,rkd->rkg', query_f, fresh_key) * score_scale
        masked = jnp.where(visible[:, None, None, :], scores, -jnp.inf)
        row_max = jnp.maximum(lax.optimization_barrier(jnp.max(masked, axis=-1)), own_score)
        weights = jnp.exp(masked - row_max[..., None])
        own_weight = jnp.exp(own_score - row_max)
        denominator = lax.optimization_barrier(jnp.sum(weights, axis=-1)) + own_weight
        rounded = lax.optimization_barrier(weights.astype(jnp.bfloat16)).astype(jnp.float32)
        own_rounded = lax.optimization_barrier(own_weight.astype(jnp.bfloat16)).astype(jnp.float32)
        numerator = jnp.einsum('rkgc,ckd->rkgd', rounded, cache_values) + own_rounded[..., None] * fresh_value[:, :, None, :]
        return (numerator / denominator[..., None]).astype(jnp.bfloat16).reshape(RPD, QH * HD)
    context = lax.map(attend, jnp.arange(blocks_total, dtype=jnp.int32)).reshape(REQS, QH * HD)
    attn_part = jnp.dot(context, w_out, preferred_element_type=jnp.float32)
    mid_rows = (tokens.astype(jnp.float32) + attn_part).astype(jnp.bfloat16)
    normed2 = rms_scale(mid_rows, ffn_gain).astype(jnp.bfloat16)
    shared = jnp.dot(swiglu_rows(normed2, shared_gate, shared_up), shared_down, preferred_element_type=jnp.float32)
    half_count = expert_gate.shape[0]
    slot_limit = REQS // TOK_DEV * MOST

    def apply_half(running, half_index):
        expert = half_index // 2
        chosen = route_idx == expert
        weight = lax.optimization_barrier(jnp.sum(jnp.where(chosen, route_wt, 0.0), axis=1))
        routed_mask = jnp.any(chosen, axis=1)
        pick_list = jnp.nonzero(routed_mask, size=slot_limit, fill_value=0)[0].astype(jnp.int32)
        live_slot = jnp.arange(slot_limit, dtype=jnp.int32) < jnp.sum(routed_mask.astype(jnp.int32))
        row_data = jnp.take(normed2, pick_list, axis=0).astype(jnp.float32)
        gate_half = lax.dynamic_index_in_dim(expert_gate, half_index, 0, keepdims=False).astype(jnp.float32)
        up_half = lax.dynamic_index_in_dim(expert_up, half_index, 0, keepdims=False).astype(jnp.float32)
        down_half = lax.dynamic_index_in_dim(expert_down, half_index, 0, keepdims=False).astype(jnp.float32)
        gate_part = jnp.dot(row_data, gate_half, precision=lax.Precision.HIGHEST)
        up_part = jnp.dot(row_data, up_half, precision=lax.Precision.HIGHEST)
        hidden = (jax.nn.silu(gate_part) * up_part).astype(jnp.bfloat16).astype(jnp.float32)
        half_out = jnp.dot(hidden, down_half, precision=lax.Precision.HIGHEST).astype(jnp.bfloat16)
        scaled = half_out.astype(jnp.float32) * jnp.where(live_slot, jnp.take(weight, pick_list), 0.0)[:, None]
        return (running.at[pick_list].add(scaled), None)
    routed, unused = lax.scan(apply_half, jnp.zeros((REQS, D), jnp.float32), jnp.arange(half_count, dtype=jnp.int32))
    result = (mid_rows.astype(jnp.float32) + shared + routed).astype(jnp.bfloat16)
    new_kv = jnp.stack([new_key.reshape(REQS, KVH * HD), new_value.reshape(REQS, KVH * HD)], axis=0)
    return (result, new_kv)
```

```python
import math

import jax
import jax.numpy as jnp
from jax import lax
from jax.experimental import pallas as pl
from jax.experimental.pallas import tpu as pltpu
from jax.sharding import PartitionSpec as P

EPS = 1e-06
ROPE_BASE = 10000.0


def rms_scale(row_data, gain):
    widened = row_data.astype(jnp.float32)
    return (
        widened
        * lax.rsqrt(jnp.mean(widened * widened, axis=-1, keepdims=True) + EPS)
        * gain.astype(jnp.float32)
    )


def rotate(vectors, positions):
    half_dim = vectors.shape[-1] // 2
    steps_idx = jnp.arange(half_dim, dtype=jnp.float32)
    frequency = jnp.exp(-(2.0 * steps_idx / vectors.shape[-1]) * math.log(ROPE_BASE))
    angles = positions.astype(jnp.float32)[:, None] * frequency[None, :]
    cosine = jnp.cos(angles)[:, None, :]
    sine_part = jnp.sin(angles)[:, None, :]
    first_half = vectors[..., :half_dim]
    second_half = vectors[..., half_dim:]
    return jnp.concatenate(
        [
            first_half * cosine - second_half * sine_part,
            second_half * cosine + first_half * sine_part,
        ],
        axis=-1,
    )


def swiglu_rows(row_data, w_gate, w_up):
    gate_part = jnp.dot(row_data, w_gate, preferred_element_type=jnp.float32)
    up_part = jnp.dot(row_data, w_up, preferred_element_type=jnp.float32)
    return (jax.nn.silu(gate_part) * up_part).astype(jnp.bfloat16)


def pick_block_rows(cap_rows):
    for rows in (1280, 1024, 1536, 768, 2048, 640, 512, 384, 256, 128):
        if cap_rows % rows == 0:
            return rows
    return cap_rows


def cache_attention(queries, row_start, row_end, row_total, own_score, start_acc, key_cache,
                    value_cache, score_scale):
    q_rows, head_dim = queries.shape
    cap_rows = key_cache.shape[0]
    block_rows = pick_block_rows(cap_rows)
    grid_steps = cap_rows // block_rows
    live_blocks = jnp.clip((row_total + block_rows - 1) // block_rows, 1, grid_steps)
    live_blocks = live_blocks.astype(jnp.int32).reshape(1)

    def kernel(nb_ref, q_ref, rs_ref, re_ref, m0_ref, acc0_ref, k_ref, v_ref, o_ref,
               m_sc, l_sc, acc_sc):
        step = pl.program_id(0)

        @pl.when(step == 0)
        def _():
            m_sc[...] = m0_ref[...]
            l_sc[...] = jnp.ones_like(l_sc)
            acc_sc[...] = acc0_ref[...]

        @pl.when(step < nb_ref[0])
        def _():
            scores = lax.dot_general(
                q_ref[...], k_ref[...], (((1,), (1,)), ((), ())),
                preferred_element_type=jnp.float32,
            ) * score_scale
            rows = step * block_rows + lax.broadcasted_iota(jnp.int32, (1, block_rows), 1)
            visible = (rows >= rs_ref[...]) & (rows < re_ref[...])
            masked = jnp.where(visible, scores, -jnp.inf)
            run_max = m_sc[...]
            new_max = jnp.maximum(run_max, jnp.max(masked, axis=1, keepdims=True))
            weights = jnp.exp(masked - new_max)
            rescale = jnp.exp(run_max - new_max)
            l_sc[...] = l_sc[...] * rescale + jnp.sum(weights, axis=1, keepdims=True)
            acc_sc[...] = acc_sc[...] * rescale + jnp.dot(
                weights.astype(jnp.bfloat16), v_ref[...], preferred_element_type=jnp.float32
            )
            m_sc[...] = new_max

        @pl.when(step == pl.num_programs(0) - 1)
        def _():
            o_ref[...] = (acc_sc[...] / l_sc[...]).astype(o_ref.dtype)

    whole = lambda step, nb: (0, 0)
    cache_block = lambda step, nb: (jnp.minimum(step, nb[0] - 1), 0)
    grid_spec = pltpu.PrefetchScalarGridSpec(
        num_scalar_prefetch=1,
        grid=(grid_steps,),
        in_specs=[
            pl.BlockSpec((q_rows, head_dim), whole),
            pl.BlockSpec((q_rows, 1), whole),
            pl.BlockSpec((q_rows, 1), whole),
            pl.BlockSpec((q_rows, 1), whole),
            pl.BlockSpec((q_rows, head_dim), whole),
            pl.BlockSpec((block_rows, head_dim), cache_block),
            pl.BlockSpec((block_rows, head_dim), cache_block),
        ],
        out_specs=pl.BlockSpec((q_rows, head_dim), whole),
        scratch_shapes=[
            pltpu.VMEM((q_rows, 1), jnp.float32),
            pltpu.VMEM((q_rows, 1), jnp.float32),
            pltpu.VMEM((q_rows, head_dim), jnp.float32),
        ],
    )
    return pl.pallas_call(
        kernel,
        grid_spec=grid_spec,
        out_shape=jax.ShapeDtypeStruct((q_rows, head_dim), jnp.bfloat16),
        compiler_params=pltpu.CompilerParams(dimension_semantics=("arbitrary",)),
    )(live_blocks, queries, row_start, row_end, own_score, start_acc, key_cache, value_cache)


def per_device(
    tokens,
    attn_gain,
    w_query,
    w_key,
    w_value,
    w_out,
    key_cache,
    value_cache,
    lengths,
    ffn_gain,
    shared_gate,
    shared_up,
    shared_down,
    expert_gate,
    expert_up,
    expert_down,
    route_idx,
    route_wt,
):
    tok_dev, model_width = tokens.shape
    heads_total = lax.axis_size("head")
    req_total = lax.axis_size("req")
    all_tok = lax.all_gather(tokens, "head", axis=0, tiled=True)
    req_dev = all_tok.shape[0]
    head_dim = w_key.shape[1]
    group_size = w_query.shape[1] // head_dim
    normed = rms_scale(all_tok, attn_gain).astype(jnp.bfloat16)
    queries = rotate(
        jnp.dot(normed, w_query, preferred_element_type=jnp.float32).reshape(
            req_dev, group_size, head_dim
        ),
        lengths,
    ).astype(jnp.bfloat16)
    new_key = rotate(
        jnp.dot(normed, w_key, preferred_element_type=jnp.float32)[:, None, :], lengths
    )[:, 0, :].astype(jnp.bfloat16)
    new_value = jnp.dot(normed, w_value, preferred_element_type=jnp.float32).astype(jnp.bfloat16)
    new_kv = jnp.stack([new_key, new_value], axis=0)
    score_scale = 1.0 / math.sqrt(head_dim)
    flat_queries = queries.reshape(req_dev * group_size, head_dim)
    own_score = (
        jnp.einsum("rgd,rd->rg", queries, new_key, preferred_element_type=jnp.float32).reshape(-1, 1)
        * score_scale
    )
    starts = jnp.cumsum(lengths) - lengths
    row_start = jnp.repeat(starts, group_size)[:, None]
    row_end = jnp.repeat(starts + lengths, group_size)[:, None]
    row_total = jnp.sum(lengths)
    start_acc = jnp.repeat(new_value, group_size, axis=0).astype(jnp.float32)
    context = cache_attention(
        flat_queries, row_start, row_end, row_total, own_score, start_acc, key_cache, value_cache,
        score_scale,
    ).reshape(req_dev, group_size * head_dim)
    slice_rows = context
    attn_part = lax.psum_scatter(
        jnp.dot(slice_rows, w_out, preferred_element_type=jnp.float32),
        "head",
        scatter_dimension=0,
        tiled=True,
    )
    mid_rows = (tokens.astype(jnp.float32) + attn_part).astype(jnp.bfloat16)
    normed_own = rms_scale(mid_rows, ffn_gain).astype(jnp.bfloat16)
    normed_all = lax.all_gather(normed_own, "head", axis=0, tiled=True)
    slice_rows = normed_all
    shared = lax.psum_scatter(
        jnp.dot(
            swiglu_rows(slice_rows, shared_gate, shared_up),
            shared_down,
            preferred_element_type=jnp.float32,
        ),
        "head",
        scatter_dimension=0,
        tiled=True,
    )
    experts_total = req_total * heads_total // 2
    top_count = route_idx.shape[1]
    pair_count = tok_dev * top_count
    most_slots = 2 * max(1, (2 * pair_count + 3 * experts_total - 1) // (3 * experts_total))
    pick_list = route_idx.reshape(pair_count)
    expert_hits = (
        pick_list[:, None] == jnp.arange(experts_total, dtype=jnp.int32)[None, :]
    ).astype(jnp.int32)
    earlier = jnp.cumsum(expert_hits, axis=0) - expert_hits
    slot_index = jnp.sum(earlier * expert_hits, axis=1)
    target = pick_list * most_slots + slot_index
    slot_place = (
        jnp.arange(experts_total * most_slots, dtype=jnp.int32)[:, None] == target[None, :]
    ).astype(jnp.bfloat16)
    token_owner = (
        jnp.arange(pair_count, dtype=jnp.int32)[:, None] // top_count
        == jnp.arange(tok_dev, dtype=jnp.int32)[None, :]
    ).astype(jnp.bfloat16)
    selector = jnp.dot(slot_place, token_owner, preferred_element_type=jnp.float32).astype(
        jnp.bfloat16
    )
    packed = (
        jnp.dot(selector, normed_own, preferred_element_type=jnp.float32)
        .astype(jnp.bfloat16)
        .reshape(experts_total, 1, most_slots, model_width)
    )
    outgoing = jnp.broadcast_to(packed, (experts_total, 2, most_slots, model_width)).reshape(
        experts_total * 2, most_slots, model_width
    )
    incoming = lax.all_to_all(outgoing, ("req", "head"), split_axis=0, concat_axis=0, tiled=True)
    item_shape = incoming.shape
    flat_rows = incoming.reshape(-1, model_width)
    hidden = swiglu_rows(flat_rows, expert_gate[0], expert_up[0])
    results = (
        jnp.dot(hidden, expert_down[0], preferred_element_type=jnp.float32)
        .astype(jnp.bfloat16)
        .reshape(item_shape)
    )
    returned = lax.all_to_all(results, ("req", "head"), split_axis=0, concat_axis=0, tiled=True)
    merged = (
        returned.reshape(experts_total, 2, most_slots, model_width)
        .astype(jnp.float32)
        .sum(axis=1)
        .reshape(experts_total * most_slots, model_width)
    )
    picked = jnp.take(merged, target, axis=0)
    routed = jnp.sum(
        (picked * route_wt.reshape(pair_count)[:, None]).reshape(tok_dev, top_count, model_width),
        axis=1,
    )
    result = (mid_rows.astype(jnp.float32) + shared + routed).astype(jnp.bfloat16)
    return (result, new_kv)


def solution(mesh):
    return jax.shard_map(
        per_device,
        mesh=mesh,
        in_specs=(
            P(("req", "head"), None),
            P(),
            P(None, "head"),
            P(None, "head"),
            P(None, "head"),
            P("head", None),
            P("req", "head"),
            P("req", "head"),
            P("req"),
            P(),
            P(None, "head"),
            P(None, "head"),
            P("head", None),
            P(("req", "head"), None, None),
            P(("req", "head"), None, None),
            P(("req", "head"), None, None),
            P(("req", "head"), None),
            P(("req", "head"), None),
        ),
        out_specs=(P(("req", "head"), None), P(None, "req", "head")),
        check_vma=False,
    )
```

```python
import math

import jax
import jax.numpy as jnp
from jax import lax
from jax.experimental import pallas as pl
from jax.experimental.pallas import tpu as pltpu
from jax.sharding import PartitionSpec as P

EPS = 1e-06
ROPE_BASE = 10000.0


def rms_scale(row_data, gain):
    widened = row_data.astype(jnp.float32)
    return (
        widened
        * lax.rsqrt(jnp.mean(widened * widened, axis=-1, keepdims=True) + EPS)
        * gain.astype(jnp.float32)
    )


def rotate(vectors, positions):
    half_dim = vectors.shape[-1] // 2
    steps_idx = jnp.arange(half_dim, dtype=jnp.float32)
    frequency = jnp.exp(-(2.0 * steps_idx / vectors.shape[-1]) * math.log(ROPE_BASE))
    angles = positions.astype(jnp.float32)[:, None] * frequency[None, :]
    cosine = jnp.cos(angles)[:, None, :]
    sine_part = jnp.sin(angles)[:, None, :]
    first_half = vectors[..., :half_dim]
    second_half = vectors[..., half_dim:]
    return jnp.concatenate(
        [
            first_half * cosine - second_half * sine_part,
            second_half * cosine + first_half * sine_part,
        ],
        axis=-1,
    )


def swiglu_rows(row_data, w_gate, w_up):
    gate_part = jnp.dot(row_data, w_gate, preferred_element_type=jnp.float32)
    up_part = jnp.dot(row_data, w_up, preferred_element_type=jnp.float32)
    return (jax.nn.silu(gate_part) * up_part).astype(jnp.bfloat16)


def pick_block_rows(cap_rows):
    for rows in (1280, 1024, 1536, 768, 2048, 640, 512, 384, 256, 128):
        if cap_rows % rows == 0:
            return rows
    return cap_rows


def cache_attention(queries, row_start, row_end, row_total, own_score, start_acc, key_cache,
                    value_cache, score_scale):
    q_rows, head_dim = queries.shape
    cap_rows = key_cache.shape[0]
    block_rows = pick_block_rows(cap_rows)
    grid_steps = cap_rows // block_rows
    live_blocks = jnp.clip((row_total + block_rows - 1) // block_rows, 1, grid_steps)
    live_blocks = live_blocks.astype(jnp.int32).reshape(1)

    def kernel(nb_ref, q_ref, rs_ref, re_ref, m0_ref, acc0_ref, k_ref, v_ref, o_ref,
               m_sc, l_sc, acc_sc):
        step = pl.program_id(0)

        @pl.when(step == 0)
        def _():
            m_sc[...] = m0_ref[...]
            l_sc[...] = jnp.ones_like(l_sc)
            acc_sc[...] = acc0_ref[...]

        @pl.when(step < nb_ref[0])
        def _():
            scores = lax.dot_general(
                q_ref[...], k_ref[...], (((1,), (1,)), ((), ())),
                preferred_element_type=jnp.float32,
            ) * score_scale
            rows = step * block_rows + lax.broadcasted_iota(jnp.int32, (1, block_rows), 1)
            visible = (rows >= rs_ref[...]) & (rows < re_ref[...])
            masked = jnp.where(visible, scores, -jnp.inf)
            run_max = m_sc[...]
            new_max = jnp.maximum(run_max, jnp.max(masked, axis=1, keepdims=True))
            weights = jnp.exp(masked - new_max)
            rescale = jnp.exp(run_max - new_max)
            l_sc[...] = l_sc[...] * rescale + jnp.sum(weights, axis=1, keepdims=True)
            acc_sc[...] = acc_sc[...] * rescale + jnp.dot(
                weights.astype(jnp.bfloat16), v_ref[...], preferred_element_type=jnp.float32
            )
            m_sc[...] = new_max

        @pl.when(step == pl.num_programs(0) - 1)
        def _():
            o_ref[...] = (acc_sc[...] / l_sc[...]).astype(o_ref.dtype)

    whole = lambda step, nb: (0, 0)
    cache_block = lambda step, nb: (jnp.minimum(step, nb[0] - 1), 0)
    grid_spec = pltpu.PrefetchScalarGridSpec(
        num_scalar_prefetch=1,
        grid=(grid_steps,),
        in_specs=[
            pl.BlockSpec((q_rows, head_dim), whole),
            pl.BlockSpec((q_rows, 1), whole),
            pl.BlockSpec((q_rows, 1), whole),
            pl.BlockSpec((q_rows, 1), whole),
            pl.BlockSpec((q_rows, head_dim), whole),
            pl.BlockSpec((block_rows, head_dim), cache_block),
            pl.BlockSpec((block_rows, head_dim), cache_block),
        ],
        out_specs=pl.BlockSpec((q_rows, head_dim), whole),
        scratch_shapes=[
            pltpu.VMEM((q_rows, 1), jnp.float32),
            pltpu.VMEM((q_rows, 1), jnp.float32),
            pltpu.VMEM((q_rows, head_dim), jnp.float32),
        ],
    )
    return pl.pallas_call(
        kernel,
        grid_spec=grid_spec,
        out_shape=jax.ShapeDtypeStruct((q_rows, head_dim), jnp.bfloat16),
        compiler_params=pltpu.CompilerParams(dimension_semantics=("arbitrary",)),
    )(live_blocks, queries, row_start, row_end, own_score, start_acc, key_cache, value_cache)


def head_shift(values, shift):
    heads = lax.axis_size("head")
    return lax.ppermute(values, "head", [(j, (j + shift) % heads) for j in range(heads)])


def gather_heads(values):
    heads = lax.axis_size("head")
    return jnp.concatenate([values] + [head_shift(values, -s) for s in range(1, heads)], axis=0)


def scatter_heads(values):
    heads = lax.axis_size("head")
    parts = values.reshape(heads, values.shape[0] // heads, *values.shape[1:])
    total = parts[0]
    for s in range(1, heads):
        total = total + head_shift(parts[s], s)
    return total


def to_rotated(values, chunk):
    heads = lax.axis_size("head")
    offset = lax.axis_index("head") * chunk
    doubled = jnp.concatenate([values, values], axis=0)
    return lax.dynamic_slice_in_dim(doubled, offset, heads * chunk, 0)


def from_rotated(values, chunk):
    heads = lax.axis_size("head")
    offset = (heads - lax.axis_index("head")) % heads * chunk
    doubled = jnp.concatenate([values, values], axis=0)
    return lax.dynamic_slice_in_dim(doubled, offset, heads * chunk, 0)


def per_device(
    tokens,
    attn_gain,
    w_query,
    w_key,
    w_value,
    w_out,
    key_cache,
    value_cache,
    lengths,
    ffn_gain,
    shared_gate,
    shared_up,
    shared_down,
    expert_gate,
    expert_up,
    expert_down,
    route_idx,
    route_wt,
):
    tok_dev, model_width = tokens.shape
    heads_total = lax.axis_size("head")
    req_total = lax.axis_size("req")
    all_tok = gather_heads(tokens)
    req_dev = all_tok.shape[0]
    head_dim = w_key.shape[1]
    group_size = w_query.shape[1] // head_dim
    starts = jnp.cumsum(lengths) - lengths
    row_total = jnp.sum(lengths)
    lengths_rot = to_rotated(lengths, tok_dev)
    starts_rot = to_rotated(starts, tok_dev)
    normed = rms_scale(all_tok, attn_gain).astype(jnp.bfloat16)
    queries = rotate(
        jnp.dot(normed, w_query, preferred_element_type=jnp.float32).reshape(
            req_dev, group_size, head_dim
        ),
        lengths_rot,
    ).astype(jnp.bfloat16)
    new_key = rotate(
        jnp.dot(normed, w_key, preferred_element_type=jnp.float32)[:, None, :], lengths_rot
    )[:, 0, :].astype(jnp.bfloat16)
    new_value = jnp.dot(normed, w_value, preferred_element_type=jnp.float32).astype(jnp.bfloat16)
    new_kv = from_rotated(jnp.stack([new_key, new_value], axis=1), tok_dev).transpose(1, 0, 2)
    score_scale = 1.0 / math.sqrt(head_dim)
    flat_queries = queries.reshape(req_dev * group_size, head_dim)
    own_score = (
        jnp.einsum("rgd,rd->rg", queries, new_key, preferred_element_type=jnp.float32).reshape(-1, 1)
        * score_scale
    )
    row_start = jnp.repeat(starts_rot, group_size)[:, None]
    row_end = jnp.repeat(starts_rot + lengths_rot, group_size)[:, None]
    start_acc = jnp.repeat(new_value, group_size, axis=0).astype(jnp.float32)
    context = cache_attention(
        flat_queries, row_start, row_end, row_total, own_score, start_acc, key_cache, value_cache,
        score_scale,
    ).reshape(req_dev, group_size * head_dim)
    attn_part = scatter_heads(jnp.dot(context, w_out, preferred_element_type=jnp.float32))
    mid_rows = (tokens.astype(jnp.float32) + attn_part).astype(jnp.bfloat16)
    normed_own = rms_scale(mid_rows, ffn_gain).astype(jnp.bfloat16)
    normed_all = gather_heads(normed_own)
    shared = scatter_heads(
        jnp.dot(
            swiglu_rows(normed_all, shared_gate, shared_up),
            shared_down,
            preferred_element_type=jnp.float32,
        )
    )
    experts_total = req_total * heads_total // 2
    top_count = route_idx.shape[1]
    pair_count = tok_dev * top_count
    most_slots = 2 * max(1, (2 * pair_count + 3 * experts_total - 1) // (3 * experts_total))
    slot_total = experts_total * most_slots
    pick_list = route_idx.reshape(pair_count)
    expert_hits = (
        pick_list[:, None] == jnp.arange(experts_total, dtype=jnp.int32)[None, :]
    ).astype(jnp.int32)
    earlier = jnp.cumsum(expert_hits, axis=0) - expert_hits
    slot_index = jnp.sum(earlier * expert_hits, axis=1)
    target = (pick_list * most_slots + slot_index).reshape(tok_dev, top_count)
    slot_hit = target[:, :, None] == jnp.arange(slot_total, dtype=jnp.int32)[None, None, :]
    selector = jnp.any(slot_hit, axis=1).T.astype(jnp.bfloat16)
    packed = (
        jnp.dot(selector, normed_own, preferred_element_type=jnp.float32)
        .astype(jnp.bfloat16)
        .reshape(experts_total, 1, most_slots, model_width)
    )
    outgoing = jnp.broadcast_to(packed, (experts_total, 2, most_slots, model_width)).reshape(
        experts_total * 2 * most_slots, model_width
    )
    incoming = lax.all_to_all(outgoing, ("req", "head"), split_axis=0, concat_axis=0, tiled=True)
    hidden = swiglu_rows(incoming, expert_gate[0], expert_up[0])
    results = jnp.dot(hidden, expert_down[0], preferred_element_type=jnp.float32).astype(
        jnp.bfloat16
    )
    returned = lax.all_to_all(results, ("req", "head"), split_axis=0, concat_axis=0, tiled=True)
    slot_weight = jnp.sum(jnp.where(slot_hit, route_wt[:, :, None], 0.0), axis=1)
    half_weight = jnp.broadcast_to(
        slot_weight.reshape(tok_dev, experts_total, 1, most_slots),
        (tok_dev, experts_total, 2, most_slots),
    ).reshape(tok_dev, experts_total * 2 * most_slots)
    routed = jnp.dot(
        half_weight,
        returned.astype(jnp.float32),
        precision=lax.Precision.HIGHEST,
        preferred_element_type=jnp.float32,
    )
    result = (mid_rows.astype(jnp.float32) + shared + routed).astype(jnp.bfloat16)
    return (result, new_kv)


def solution(mesh):
    return jax.shard_map(
        per_device,
        mesh=mesh,
        in_specs=(
            P(("req", "head"), None),
            P(),
            P(None, "head"),
            P(None, "head"),
            P(None, "head"),
            P("head", None),
            P("req", "head"),
            P("req", "head"),
            P("req"),
            P(),
            P(None, "head"),
            P(None, "head"),
            P("head", None),
            P(("req", "head"), None, None),
            P(("req", "head"), None, None),
            P(("req", "head"), None, None),
            P(("req", "head"), None),
            P(("req", "head"), None),
        ),
        out_specs=(P(("req", "head"), None), P(None, "req", "head")),
        check_vma=False,
    )
```

```python
import math

import jax
import jax.numpy as jnp
from jax import lax
from jax.experimental import pallas as pl
from jax.experimental.pallas import tpu as pltpu
from jax.sharding import PartitionSpec as P

EPS = 1e-06
ROPE_BASE = 10000.0


def rms_scale(row_data, gain):
    widened = row_data.astype(jnp.float32)
    return (
        widened
        * lax.rsqrt(jnp.mean(widened * widened, axis=-1, keepdims=True) + EPS)
        * gain.astype(jnp.float32)
    )


def rotate(vectors, positions):
    half_dim = vectors.shape[-1] // 2
    steps_idx = jnp.arange(half_dim, dtype=jnp.float32)
    frequency = jnp.exp(-(2.0 * steps_idx / vectors.shape[-1]) * math.log(ROPE_BASE))
    angles = positions.astype(jnp.float32)[:, None] * frequency[None, :]
    cosine = jnp.cos(angles)[:, None, :]
    sine_part = jnp.sin(angles)[:, None, :]
    first_half = vectors[..., :half_dim]
    second_half = vectors[..., half_dim:]
    return jnp.concatenate(
        [
            first_half * cosine - second_half * sine_part,
            second_half * cosine + first_half * sine_part,
        ],
        axis=-1,
    )


def swiglu_rows(row_data, w_gate, w_up):
    gate_part = jnp.dot(row_data, w_gate, preferred_element_type=jnp.float32)
    up_part = jnp.dot(row_data, w_up, preferred_element_type=jnp.float32)
    return (jax.nn.silu(gate_part) * up_part).astype(jnp.bfloat16)


def pick_block_rows(cap_rows):
    for rows in (2432, 2560, 2048, 1920, 2304, 1280, 1024, 768, 640, 512, 384, 256, 128):
        if cap_rows % rows == 0:
            return rows
    return cap_rows


def cache_attention(queries, row_start, row_end, row_total, own_score, start_acc, key_cache,
                    value_cache, score_scale, tile_rows, tile_lo, tile_hi):
    q_rows, head_dim = queries.shape
    cap_rows = key_cache.shape[0]
    block_rows = pick_block_rows(cap_rows)
    grid_steps = cap_rows // block_rows
    tile_count = q_rows // tile_rows
    live_blocks = jnp.clip((row_total + block_rows - 1) // block_rows, 1, grid_steps)
    table = jnp.concatenate(
        [live_blocks.astype(jnp.int32).reshape(1), tile_lo.astype(jnp.int32),
         tile_hi.astype(jnp.int32)]
    )

    def kernel(tab_ref, q_ref, rs_ref, re_ref, m0_ref, acc0_ref, k_ref, v_ref, o_ref,
               m_sc, l_sc, acc_sc):
        step = pl.program_id(0)
        block_lo = step * block_rows

        @pl.when(step == 0)
        def _():
            m_sc[...] = m0_ref[...]
            l_sc[...] = jnp.ones_like(l_sc)
            acc_sc[...] = acc0_ref[...]

        for tile in range(tile_count):
            rows_of = pl.ds(tile * tile_rows, tile_rows)
            meets = (
                (step < tab_ref[0])
                & (tab_ref[1 + tile] < block_lo + block_rows)
                & (tab_ref[1 + tile_count + tile] > block_lo)
            )

            @pl.when(meets)
            def _():
                scores = lax.dot_general(
                    q_ref[rows_of, :], k_ref[...], (((1,), (1,)), ((), ())),
                    preferred_element_type=jnp.float32,
                ) * score_scale
                rows = block_lo + lax.broadcasted_iota(jnp.int32, (1, block_rows), 1)
                visible = (rows >= rs_ref[rows_of, :]) & (rows < re_ref[rows_of, :])
                masked = jnp.where(visible, scores, -jnp.inf)
                run_max = m_sc[rows_of, :]
                new_max = jnp.maximum(run_max, jnp.max(masked, axis=1, keepdims=True))
                weights = jnp.exp(masked - new_max)
                rescale = jnp.exp(run_max - new_max)
                l_sc[rows_of, :] = l_sc[rows_of, :] * rescale + jnp.sum(weights, axis=1, keepdims=True)
                acc_sc[rows_of, :] = acc_sc[rows_of, :] * rescale + jnp.dot(
                    weights.astype(jnp.bfloat16), v_ref[...], preferred_element_type=jnp.float32
                )
                m_sc[rows_of, :] = new_max

        @pl.when(step == pl.num_programs(0) - 1)
        def _():
            o_ref[...] = (acc_sc[...] / l_sc[...]).astype(o_ref.dtype)

    whole = lambda step, tab: (0, 0)
    cache_block = lambda step, tab: (jnp.minimum(step, tab[0] - 1), 0)
    grid_spec = pltpu.PrefetchScalarGridSpec(
        num_scalar_prefetch=1,
        grid=(grid_steps,),
        in_specs=[
            pl.BlockSpec((q_rows, head_dim), whole),
            pl.BlockSpec((q_rows, 1), whole),
            pl.BlockSpec((q_rows, 1), whole),
            pl.BlockSpec((q_rows, 1), whole),
            pl.BlockSpec((q_rows, head_dim), whole),
            pl.BlockSpec((block_rows, head_dim), cache_block),
            pl.BlockSpec((block_rows, head_dim), cache_block),
        ],
        out_specs=pl.BlockSpec((q_rows, head_dim), whole),
        scratch_shapes=[
            pltpu.VMEM((q_rows, 1), jnp.float32),
            pltpu.VMEM((q_rows, 1), jnp.float32),
            pltpu.VMEM((q_rows, head_dim), jnp.float32),
        ],
    )
    return pl.pallas_call(
        kernel,
        grid_spec=grid_spec,
        out_shape=jax.ShapeDtypeStruct((q_rows, head_dim), jnp.bfloat16),
        compiler_params=pltpu.CompilerParams(dimension_semantics=("arbitrary",)),
    )(table, queries, row_start, row_end, own_score, start_acc, key_cache, value_cache)


def head_shift(values, shift):
    heads = lax.axis_size("head")
    return lax.ppermute(values, "head", [(j, (j + shift) % heads) for j in range(heads)])


def gather_heads(values):
    heads = lax.axis_size("head")
    return jnp.concatenate([values] + [head_shift(values, -s) for s in range(1, heads)], axis=0)


def scatter_heads(values):
    heads = lax.axis_size("head")
    parts = values.reshape(heads, values.shape[0] // heads, *values.shape[1:])
    total = parts[0]
    for s in range(1, heads):
        total = total + head_shift(parts[s], s)
    return total


def to_rotated(values, chunk):
    heads = lax.axis_size("head")
    offset = lax.axis_index("head") * chunk
    doubled = jnp.concatenate([values, values], axis=0)
    return lax.dynamic_slice_in_dim(doubled, offset, heads * chunk, 0)


def from_rotated(values, chunk):
    heads = lax.axis_size("head")
    offset = (heads - lax.axis_index("head")) % heads * chunk
    doubled = jnp.concatenate([values, values], axis=0)
    return lax.dynamic_slice_in_dim(doubled, offset, heads * chunk, 0)


def per_device(
    tokens,
    attn_gain,
    w_query,
    w_key,
    w_value,
    w_out,
    key_cache,
    value_cache,
    lengths,
    ffn_gain,
    shared_gate,
    shared_up,
    shared_down,
    expert_gate,
    expert_up,
    expert_down,
    route_idx,
    route_wt,
):
    tok_dev, model_width = tokens.shape
    heads_total = lax.axis_size("head")
    req_total = lax.axis_size("req")
    all_tok = gather_heads(tokens)
    req_dev = all_tok.shape[0]
    head_dim = w_key.shape[1]
    group_size = w_query.shape[1] // head_dim
    starts = jnp.cumsum(lengths) - lengths
    row_total = jnp.sum(lengths)
    lengths_rot = to_rotated(lengths, tok_dev)
    starts_rot = to_rotated(starts, tok_dev)
    normed = rms_scale(all_tok, attn_gain).astype(jnp.bfloat16)
    queries = rotate(
        jnp.dot(normed, w_query, preferred_element_type=jnp.float32).reshape(
            req_dev, group_size, head_dim
        ),
        lengths_rot,
    ).astype(jnp.bfloat16)
    new_key = rotate(
        jnp.dot(normed, w_key, preferred_element_type=jnp.float32)[:, None, :], lengths_rot
    )[:, 0, :].astype(jnp.bfloat16)
    new_value = jnp.dot(normed, w_value, preferred_element_type=jnp.float32).astype(jnp.bfloat16)
    new_kv = from_rotated(jnp.stack([new_key, new_value], axis=1), tok_dev).transpose(1, 0, 2)
    score_scale = 1.0 / math.sqrt(head_dim)
    flat_queries = queries.reshape(req_dev * group_size, head_dim)
    own_score = (
        jnp.einsum("rgd,rd->rg", queries, new_key, preferred_element_type=jnp.float32).reshape(-1, 1)
        * score_scale
    )
    row_start = jnp.repeat(starts_rot, group_size)[:, None]
    row_end = jnp.repeat(starts_rot + lengths_rot, group_size)[:, None]
    start_acc = jnp.repeat(new_value, group_size, axis=0).astype(jnp.float32)
    tile_reqs = 8 if req_dev % 8 == 0 else req_dev
    ends_rot = starts_rot + lengths_rot
    context = cache_attention(
        flat_queries, row_start, row_end, row_total, own_score, start_acc, key_cache, value_cache,
        score_scale, tile_reqs * group_size,
        jnp.min(starts_rot.reshape(-1, tile_reqs), axis=1),
        jnp.max(ends_rot.reshape(-1, tile_reqs), axis=1),
    ).reshape(req_dev, group_size * head_dim)
    attn_part = scatter_heads(jnp.dot(context, w_out, preferred_element_type=jnp.float32))
    mid_rows = (tokens.astype(jnp.float32) + attn_part).astype(jnp.bfloat16)
    normed_own = rms_scale(mid_rows, ffn_gain).astype(jnp.bfloat16)
    normed_all = gather_heads(normed_own)
    shared = scatter_heads(
        jnp.dot(
            swiglu_rows(normed_all, shared_gate, shared_up),
            shared_down,
            preferred_element_type=jnp.float32,
        )
    )
    experts_total = req_total * heads_total // 2
    top_count = route_idx.shape[1]
    pair_count = tok_dev * top_count
    most_slots = 2 * max(1, (2 * pair_count + 3 * experts_total - 1) // (3 * experts_total))
    slot_total = experts_total * most_slots
    pick_list = route_idx.reshape(pair_count)
    expert_hits = (
        pick_list[:, None] == jnp.arange(experts_total, dtype=jnp.int32)[None, :]
    ).astype(jnp.int32)
    earlier = jnp.cumsum(expert_hits, axis=0) - expert_hits
    slot_index = jnp.sum(earlier * expert_hits, axis=1)
    target = (pick_list * most_slots + slot_index).reshape(tok_dev, top_count)
    slot_hit = target[:, :, None] == jnp.arange(slot_total, dtype=jnp.int32)[None, None, :]
    selector = jnp.any(slot_hit, axis=1).T.astype(jnp.bfloat16)
    packed = (
        jnp.dot(selector, normed_own, preferred_element_type=jnp.float32)
        .astype(jnp.bfloat16)
        .reshape(experts_total, 1, most_slots, model_width)
    )
    outgoing = jnp.broadcast_to(packed, (experts_total, 2, most_slots, model_width)).reshape(
        experts_total * 2 * most_slots, model_width
    )
    incoming = lax.all_to_all(outgoing, ("req", "head"), split_axis=0, concat_axis=0, tiled=True)
    hidden = swiglu_rows(incoming, expert_gate[0], expert_up[0])
    results = jnp.dot(hidden, expert_down[0], preferred_element_type=jnp.float32).astype(
        jnp.bfloat16
    )
    returned = lax.all_to_all(results, ("req", "head"), split_axis=0, concat_axis=0, tiled=True)
    slot_weight = jnp.sum(jnp.where(slot_hit, route_wt[:, :, None], 0.0), axis=1)
    half_weight = jnp.broadcast_to(
        slot_weight.reshape(tok_dev, experts_total, 1, most_slots),
        (tok_dev, experts_total, 2, most_slots),
    ).reshape(tok_dev, experts_total * 2 * most_slots)
    routed = jnp.dot(
        half_weight,
        returned.astype(jnp.float32),
        precision=lax.Precision.HIGHEST,
        preferred_element_type=jnp.float32,
    )
    result = (mid_rows.astype(jnp.float32) + shared + routed).astype(jnp.bfloat16)
    return (result, new_kv)


def solution(mesh):
    return jax.shard_map(
        per_device,
        mesh=mesh,
        in_specs=(
            P(("req", "head"), None),
            P(),
            P(None, "head"),
            P(None, "head"),
            P(None, "head"),
            P("head", None),
            P("req", "head"),
            P("req", "head"),
            P("req"),
            P(),
            P(None, "head"),
            P(None, "head"),
            P("head", None),
            P(("req", "head"), None, None),
            P(("req", "head"), None, None),
            P(("req", "head"), None, None),
            P(("req", "head"), None),
            P(("req", "head"), None),
        ),
        out_specs=(P(("req", "head"), None), P(None, "req", "head")),
        check_vma=False,
    )
```

```python
import math

import jax
import jax.numpy as jnp
from jax import lax
from jax.experimental import pallas as pl
from jax.experimental.pallas import tpu as pltpu
from jax.sharding import PartitionSpec as P

EPS = 1e-06
ROPE_BASE = 10000.0


def rms_scale(row_data, gain):
    widened = row_data.astype(jnp.float32)
    return (
        widened
        * lax.rsqrt(jnp.mean(widened * widened, axis=-1, keepdims=True) + EPS)
        * gain.astype(jnp.float32)
    )


def rotate(vectors, positions):
    half_dim = vectors.shape[-1] // 2
    steps_idx = jnp.arange(half_dim, dtype=jnp.float32)
    frequency = jnp.exp(-(2.0 * steps_idx / vectors.shape[-1]) * math.log(ROPE_BASE))
    angles = positions.astype(jnp.float32)[:, None] * frequency[None, :]
    cosine = jnp.cos(angles)[:, None, :]
    sine_part = jnp.sin(angles)[:, None, :]
    first_half = vectors[..., :half_dim]
    second_half = vectors[..., half_dim:]
    return jnp.concatenate(
        [
            first_half * cosine - second_half * sine_part,
            second_half * cosine + first_half * sine_part,
        ],
        axis=-1,
    )


def swiglu_rows(row_data, w_gate, w_up):
    gate_part = jnp.dot(row_data, w_gate, preferred_element_type=jnp.float32)
    up_part = jnp.dot(row_data, w_up, preferred_element_type=jnp.float32)
    return (jax.nn.silu(gate_part) * up_part).astype(jnp.bfloat16)


def pick_block_rows(cap_rows):
    for rows in (2432, 2560, 2048, 1920, 2304, 1280, 1024, 768, 640, 512, 384, 256, 128):
        if cap_rows % rows == 0:
            return rows
    return cap_rows


def cache_attention(queries, row_start, row_end, row_total, own_score, start_acc, key_cache,
                    value_cache, score_scale, tile_rows, tile_lo, tile_hi):
    q_rows, head_dim = queries.shape
    cap_rows = key_cache.shape[0]
    block_rows = pick_block_rows(cap_rows)
    grid_steps = cap_rows // block_rows
    tile_count = q_rows // tile_rows
    live_blocks = jnp.clip((row_total + block_rows - 1) // block_rows, 1, grid_steps)
    table = jnp.concatenate(
        [live_blocks.astype(jnp.int32).reshape(1), tile_lo.astype(jnp.int32),
         tile_hi.astype(jnp.int32)]
    )

    def kernel(tab_ref, q_ref, rs_ref, re_ref, m0_ref, acc0_ref, k_ref, v_ref, o_ref,
               m_sc, l_sc, acc_sc):
        step = pl.program_id(0)
        block_lo = step * block_rows

        @pl.when(step == 0)
        def _():
            m_sc[...] = m0_ref[...]
            l_sc[...] = jnp.ones_like(l_sc)
            acc_sc[...] = acc0_ref[...]

        for tile in range(tile_count):
            rows_of = pl.ds(tile * tile_rows, tile_rows)
            meets = (
                (step < tab_ref[0])
                & (tab_ref[1 + tile] < block_lo + block_rows)
                & (tab_ref[1 + tile_count + tile] > block_lo)
            )

            @pl.when(meets)
            def _():
                scores = lax.dot_general(
                    q_ref[rows_of, :], k_ref[...], (((1,), (1,)), ((), ())),
                    preferred_element_type=jnp.float32,
                ) * score_scale
                rows = block_lo + lax.broadcasted_iota(jnp.int32, (1, block_rows), 1)
                visible = (rows >= rs_ref[rows_of, :]) & (rows < re_ref[rows_of, :])
                masked = jnp.where(visible, scores, -jnp.inf)
                run_max = m_sc[rows_of, :]
                new_max = jnp.maximum(run_max, jnp.max(masked, axis=1, keepdims=True))
                weights = jnp.exp(masked - new_max)
                rescale = jnp.exp(run_max - new_max)
                l_sc[rows_of, :] = l_sc[rows_of, :] * rescale + jnp.sum(weights, axis=1, keepdims=True)
                acc_sc[rows_of, :] = acc_sc[rows_of, :] * rescale + jnp.dot(
                    weights.astype(jnp.bfloat16), v_ref[...], preferred_element_type=jnp.float32
                )
                m_sc[rows_of, :] = new_max

        @pl.when(step == pl.num_programs(0) - 1)
        def _():
            o_ref[...] = (acc_sc[...] / l_sc[...]).astype(o_ref.dtype)

    whole = lambda step, tab: (0, 0)
    cache_block = lambda step, tab: (jnp.minimum(step, tab[0] - 1), 0)
    grid_spec = pltpu.PrefetchScalarGridSpec(
        num_scalar_prefetch=1,
        grid=(grid_steps,),
        in_specs=[
            pl.BlockSpec((q_rows, head_dim), whole),
            pl.BlockSpec((q_rows, 1), whole),
            pl.BlockSpec((q_rows, 1), whole),
            pl.BlockSpec((q_rows, 1), whole),
            pl.BlockSpec((q_rows, head_dim), whole),
            pl.BlockSpec((block_rows, head_dim), cache_block),
            pl.BlockSpec((block_rows, head_dim), cache_block),
        ],
        out_specs=pl.BlockSpec((q_rows, head_dim), whole),
        scratch_shapes=[
            pltpu.VMEM((q_rows, 1), jnp.float32),
            pltpu.VMEM((q_rows, 1), jnp.float32),
            pltpu.VMEM((q_rows, head_dim), jnp.float32),
        ],
    )
    return pl.pallas_call(
        kernel,
        grid_spec=grid_spec,
        out_shape=jax.ShapeDtypeStruct((q_rows, head_dim), jnp.bfloat16),
        compiler_params=pltpu.CompilerParams(dimension_semantics=("arbitrary",)),
    )(table, queries, row_start, row_end, own_score, start_acc, key_cache, value_cache)


def head_shift(values, shift):
    heads = lax.axis_size("head")
    return lax.ppermute(values, "head", [(j, (j + shift) % heads) for j in range(heads)])


def gather_heads(values):
    heads = lax.axis_size("head")
    return jnp.concatenate([values] + [head_shift(values, -s) for s in range(1, heads)], axis=0)


def scatter_heads(values):
    heads = lax.axis_size("head")
    parts = values.reshape(heads, values.shape[0] // heads, *values.shape[1:])
    total = parts[0]
    for s in range(1, heads):
        total = total + head_shift(parts[s], s)
    return total


def to_rotated(values, chunk):
    heads = lax.axis_size("head")
    offset = lax.axis_index("head") * chunk
    doubled = jnp.concatenate([values, values], axis=0)
    return lax.dynamic_slice_in_dim(doubled, offset, heads * chunk, 0)


def from_rotated(values, chunk):
    heads = lax.axis_size("head")
    offset = (heads - lax.axis_index("head")) % heads * chunk
    doubled = jnp.concatenate([values, values], axis=0)
    return lax.dynamic_slice_in_dim(doubled, offset, heads * chunk, 0)


def per_device(
    tokens,
    attn_gain,
    w_query,
    w_key,
    w_value,
    w_out,
    key_cache,
    value_cache,
    lengths,
    ffn_gain,
    shared_gate,
    shared_up,
    shared_down,
    expert_gate,
    expert_up,
    expert_down,
    route_idx,
    route_wt,
):
    tok_dev, model_width = tokens.shape
    heads_total = lax.axis_size("head")
    req_total = lax.axis_size("req")
    all_tok = gather_heads(tokens)
    req_dev = all_tok.shape[0]
    head_dim = w_key.shape[1]
    group_size = w_query.shape[1] // head_dim
    starts = jnp.cumsum(lengths) - lengths
    row_total = jnp.sum(lengths)
    lengths_rot = to_rotated(lengths, tok_dev)
    starts_rot = to_rotated(starts, tok_dev)
    normed = rms_scale(all_tok, attn_gain).astype(jnp.bfloat16)
    queries = rotate(
        jnp.dot(normed, w_query, preferred_element_type=jnp.float32).reshape(
            req_dev, group_size, head_dim
        ),
        lengths_rot,
    ).astype(jnp.bfloat16)
    new_key = rotate(
        jnp.dot(normed, w_key, preferred_element_type=jnp.float32)[:, None, :], lengths_rot
    )[:, 0, :].astype(jnp.bfloat16)
    new_value = jnp.dot(normed, w_value, preferred_element_type=jnp.float32).astype(jnp.bfloat16)
    new_kv = from_rotated(jnp.stack([new_key, new_value], axis=1), tok_dev).transpose(1, 0, 2)
    score_scale = 1.0 / math.sqrt(head_dim)
    flat_queries = queries.reshape(req_dev * group_size, head_dim)
    own_score = (
        jnp.einsum("rgd,rd->rg", queries, new_key, preferred_element_type=jnp.float32).reshape(-1, 1)
        * score_scale
    )
    row_start = jnp.repeat(starts_rot, group_size)[:, None]
    row_end = jnp.repeat(starts_rot + lengths_rot, group_size)[:, None]
    start_acc = jnp.repeat(new_value, group_size, axis=0).astype(jnp.float32)
    tile_reqs = 8 if req_dev % 8 == 0 else req_dev
    ends_rot = starts_rot + lengths_rot
    context = cache_attention(
        flat_queries, row_start, row_end, row_total, own_score, start_acc, key_cache, value_cache,
        score_scale, tile_reqs * group_size,
        jnp.min(starts_rot.reshape(-1, tile_reqs), axis=1),
        jnp.max(ends_rot.reshape(-1, tile_reqs), axis=1),
    ).reshape(req_dev, group_size * head_dim)
    attn_part = scatter_heads(jnp.dot(context, w_out, preferred_element_type=jnp.float32))
    mid_rows = (tokens.astype(jnp.float32) + attn_part).astype(jnp.bfloat16)
    normed_own = rms_scale(mid_rows, ffn_gain).astype(jnp.bfloat16)
    normed_all = gather_heads(normed_own)
    experts_total = req_total * heads_total // 2
    top_count = route_idx.shape[1]
    pair_count = tok_dev * top_count
    most_slots = 2 * max(1, (2 * pair_count + 3 * experts_total - 1) // (3 * experts_total))
    group_slots = heads_total * most_slots
    slot_total = req_total * group_slots
    idx_all = gather_heads(route_idx)
    wt_all = gather_heads(route_wt)
    picks = idx_all.reshape(heads_total, pair_count)
    expert_hits = (
        picks[:, :, None] == jnp.arange(experts_total, dtype=jnp.int32)[None, None, :]
    ).astype(jnp.int32)
    earlier = jnp.cumsum(expert_hits, axis=1) - expert_hits
    local_slot = jnp.sum(earlier * expert_hits, axis=2)
    my_head = lax.axis_index("head")
    owner = 2 * picks + my_head % 2
    part = jnp.arange(heads_total, dtype=jnp.int32)[:, None]
    target = jnp.where(
        owner % heads_total == my_head,
        owner // heads_total * group_slots + part * most_slots + local_slot,
        -1,
    ).reshape(req_dev, top_count)
    slot_hit = target[:, :, None] == jnp.arange(slot_total, dtype=jnp.int32)[None, None, :]
    selector = jnp.any(slot_hit, axis=1).T.astype(jnp.bfloat16)
    packed = jnp.dot(selector, normed_all, preferred_element_type=jnp.float32).astype(jnp.bfloat16)
    incoming = lax.all_to_all(packed, "req", split_axis=0, concat_axis=0, tiled=True)
    hidden = swiglu_rows(incoming, expert_gate[0], expert_up[0])
    results = jnp.dot(hidden, expert_down[0], preferred_element_type=jnp.float32).astype(
        jnp.bfloat16
    )
    returned = lax.all_to_all(results, "req", split_axis=0, concat_axis=0, tiled=True)
    slot_weight = jnp.sum(jnp.where(slot_hit, wt_all[:, :, None], 0.0), axis=1)
    routed_part = jnp.dot(
        slot_weight,
        returned.astype(jnp.float32),
        precision=lax.Precision.HIGHEST,
        preferred_element_type=jnp.float32,
    )
    shared_part = jnp.dot(
        swiglu_rows(normed_all, shared_gate, shared_up),
        shared_down,
        preferred_element_type=jnp.float32,
    )
    ffn_out = scatter_heads(shared_part + routed_part)
    result = (mid_rows.astype(jnp.float32) + ffn_out).astype(jnp.bfloat16)
    return (result, new_kv)


def solution(mesh):
    return jax.shard_map(
        per_device,
        mesh=mesh,
        in_specs=(
            P(("req", "head"), None),
            P(),
            P(None, "head"),
            P(None, "head"),
            P(None, "head"),
            P("head", None),
            P("req", "head"),
            P("req", "head"),
            P("req"),
            P(),
            P(None, "head"),
            P(None, "head"),
            P("head", None),
            P(("req", "head"), None, None),
            P(("req", "head"), None, None),
            P(("req", "head"), None, None),
            P(("req", "head"), None),
            P(("req", "head"), None),
        ),
        out_specs=(P(("req", "head"), None), P(None, "req", "head")),
        check_vma=False,
    )
```

```python
import math

import jax
import jax.numpy as jnp
from jax import lax
from jax.experimental import pallas as pl
from jax.experimental.pallas import tpu as pltpu
from jax.sharding import PartitionSpec as P


EPS = 1e-06
ROPE_BASE = 10000.0


def rms_scale(row_data, gain):
    widened = row_data.astype(jnp.float32)
    return (
        widened
        * lax.rsqrt(jnp.mean(widened * widened, axis=-1, keepdims=True) + EPS)
        * gain.astype(jnp.float32)
    )


def rotate(vectors, positions):
    half_dim = vectors.shape[-1] // 2
    steps_idx = jnp.arange(half_dim, dtype=jnp.float32)
    frequency = jnp.exp(-(2.0 * steps_idx / vectors.shape[-1]) * math.log(ROPE_BASE))
    angles = positions.astype(jnp.float32)[:, None] * frequency[None, :]
    cosine = jnp.cos(angles)[:, None, :]
    sine_part = jnp.sin(angles)[:, None, :]
    first_half = vectors[..., :half_dim]
    second_half = vectors[..., half_dim:]
    return jnp.concatenate(
        [
            first_half * cosine - second_half * sine_part,
            second_half * cosine + first_half * sine_part,
        ],
        axis=-1,
    )


def swiglu_rows(row_data, w_gate, w_up):
    gate_part = jnp.dot(row_data, w_gate, preferred_element_type=jnp.float32)
    up_part = jnp.dot(row_data, w_up, preferred_element_type=jnp.float32)
    return (jax.nn.silu(gate_part) * up_part).astype(jnp.bfloat16)


def pick_block_rows(cap_rows):
    for rows in (4864, 4096, 5120, 3840, 2432, 2560, 2048, 1920, 1280, 1024, 640, 512, 256, 128):
        if cap_rows % rows == 0:
            return rows
    return cap_rows


def cache_attention(queries, row_start, row_end, row_total, own_score, start_acc, key_cache,
                    value_cache, score_scale, tile_rows, tile_lo, tile_hi):
    q_rows, head_dim = queries.shape
    cap_rows = key_cache.shape[0]
    block_rows = pick_block_rows(cap_rows)
    grid_steps = cap_rows // block_rows
    tile_count = q_rows // tile_rows
    live_blocks = jnp.clip((row_total + block_rows - 1) // block_rows, 1, grid_steps)
    table = jnp.concatenate(
        [live_blocks.astype(jnp.int32).reshape(1), tile_lo.astype(jnp.int32),
         tile_hi.astype(jnp.int32)]
    )

    def kernel(tab_ref, q_ref, rs_ref, re_ref, m0_ref, acc0_ref, k_ref, v_ref, o_ref,
               m_sc, l_sc, acc_sc):
        step = pl.program_id(0)
        block_lo = step * block_rows

        @pl.when(step == 0)
        def _():
            m_sc[...] = m0_ref[...]
            l_sc[...] = jnp.ones_like(l_sc)
            acc_sc[...] = acc0_ref[...]

        for tile in range(tile_count):
            rows_of = pl.ds(tile * tile_rows, tile_rows)
            meets = (
                (step < tab_ref[0])
                & (tab_ref[1 + tile] < block_lo + block_rows)
                & (tab_ref[1 + tile_count + tile] > block_lo)
            )

            @pl.when(meets)
            def _():
                scores = lax.dot_general(
                    q_ref[rows_of, :], k_ref[...], (((1,), (1,)), ((), ())),
                    preferred_element_type=jnp.float32,
                ) * score_scale
                rows = block_lo + lax.broadcasted_iota(jnp.int32, (1, block_rows), 1)
                visible = (rows >= rs_ref[rows_of, :]) & (rows < re_ref[rows_of, :])
                masked = jnp.where(visible, scores, -jnp.inf)
                run_max = m_sc[rows_of, :]
                new_max = jnp.maximum(run_max, jnp.max(masked, axis=1, keepdims=True))
                weights = jnp.exp(masked - new_max)
                rescale = jnp.exp(run_max - new_max)
                l_sc[rows_of, :] = l_sc[rows_of, :] * rescale + jnp.sum(weights, axis=1, keepdims=True)
                acc_sc[rows_of, :] = acc_sc[rows_of, :] * rescale + jnp.dot(
                    weights.astype(jnp.bfloat16), v_ref[...], preferred_element_type=jnp.float32
                )
                m_sc[rows_of, :] = new_max

        @pl.when(step == pl.num_programs(0) - 1)
        def _():
            o_ref[...] = (acc_sc[...] / l_sc[...]).astype(o_ref.dtype)

    whole = lambda step, tab: (0, 0)
    cache_block = lambda step, tab: (jnp.minimum(step, tab[0] - 1), 0)
    grid_spec = pltpu.PrefetchScalarGridSpec(
        num_scalar_prefetch=1,
        grid=(grid_steps,),
        in_specs=[
            pl.BlockSpec((q_rows, head_dim), whole),
            pl.BlockSpec((q_rows, 1), whole),
            pl.BlockSpec((q_rows, 1), whole),
            pl.BlockSpec((q_rows, 1), whole),
            pl.BlockSpec((q_rows, head_dim), whole),
            pl.BlockSpec((block_rows, head_dim), cache_block),
            pl.BlockSpec((block_rows, head_dim), cache_block),
        ],
        out_specs=pl.BlockSpec((q_rows, head_dim), whole),
        scratch_shapes=[
            pltpu.VMEM((q_rows, 1), jnp.float32),
            pltpu.VMEM((q_rows, 1), jnp.float32),
            pltpu.VMEM((q_rows, head_dim), jnp.float32),
        ],
    )
    return pl.pallas_call(
        kernel,
        grid_spec=grid_spec,
        out_shape=jax.ShapeDtypeStruct((q_rows, head_dim), jnp.bfloat16),
        compiler_params=pltpu.CompilerParams(dimension_semantics=("arbitrary",)),
    )(table, queries, row_start, row_end, own_score, start_acc, key_cache, value_cache)


def head_shift(values, shift):
    heads = lax.axis_size("head")
    return lax.ppermute(values, "head", [(j, (j + shift) % heads) for j in range(heads)])


def gather_heads(values):
    heads = lax.axis_size("head")
    return jnp.concatenate([values] + [head_shift(values, -s) for s in range(1, heads)], axis=0)


def scatter_heads(values):
    heads = lax.axis_size("head")
    parts = values.reshape(heads, values.shape[0] // heads, *values.shape[1:])
    total = parts[0]
    for s in range(1, heads):
        total = total + head_shift(parts[s], s)
    return total


def to_rotated(values, chunk):
    heads = lax.axis_size("head")
    offset = lax.axis_index("head") * chunk
    doubled = jnp.concatenate([values, values], axis=0)
    return lax.dynamic_slice_in_dim(doubled, offset, heads * chunk, 0)


def from_rotated(values, chunk):
    heads = lax.axis_size("head")
    offset = (heads - lax.axis_index("head")) % heads * chunk
    doubled = jnp.concatenate([values, values], axis=0)
    return lax.dynamic_slice_in_dim(doubled, offset, heads * chunk, 0)


def per_device(
    tokens,
    attn_gain,
    w_query,
    w_key,
    w_value,
    w_out,
    key_cache,
    value_cache,
    lengths,
    ffn_gain,
    shared_gate,
    shared_up,
    shared_down,
    expert_gate,
    expert_up,
    expert_down,
    route_idx,
    route_wt,
):
    tok_dev, model_width = tokens.shape
    heads_total = lax.axis_size("head")
    req_total = lax.axis_size("req")
    all_tok = gather_heads(tokens)
    req_dev = all_tok.shape[0]
    head_dim = w_key.shape[1]
    group_size = w_query.shape[1] // head_dim
    starts = jnp.cumsum(lengths) - lengths
    row_total = jnp.sum(lengths)
    lengths_rot = to_rotated(lengths, tok_dev)
    starts_rot = to_rotated(starts, tok_dev)
    normed = rms_scale(all_tok, attn_gain).astype(jnp.bfloat16)
    queries = rotate(
        jnp.dot(normed, w_query, preferred_element_type=jnp.float32).reshape(
            req_dev, group_size, head_dim
        ),
        lengths_rot,
    ).astype(jnp.bfloat16)
    new_key = rotate(
        jnp.dot(normed, w_key, preferred_element_type=jnp.float32)[:, None, :], lengths_rot
    )[:, 0, :].astype(jnp.bfloat16)
    new_value = jnp.dot(normed, w_value, preferred_element_type=jnp.float32).astype(jnp.bfloat16)
    new_kv = from_rotated(jnp.stack([new_key, new_value], axis=1), tok_dev).transpose(1, 0, 2)
    score_scale = 1.0 / math.sqrt(head_dim)
    flat_queries = queries.reshape(req_dev * group_size, head_dim)
    own_score = (
        jnp.einsum("rgd,rd->rg", queries, new_key, preferred_element_type=jnp.float32).reshape(-1, 1)
        * score_scale
    )
    row_start = jnp.repeat(starts_rot, group_size)[:, None]
    row_end = jnp.repeat(starts_rot + lengths_rot, group_size)[:, None]
    start_acc = jnp.repeat(new_value, group_size, axis=0).astype(jnp.float32)
    tile_reqs = 16 if req_dev % 16 == 0 else req_dev
    ends_rot = starts_rot + lengths_rot
    context = cache_attention(
        flat_queries, row_start, row_end, row_total, own_score, start_acc, key_cache, value_cache,
        score_scale, tile_reqs * group_size,
        jnp.min(starts_rot.reshape(-1, tile_reqs), axis=1),
        jnp.max(ends_rot.reshape(-1, tile_reqs), axis=1),
    ).reshape(req_dev, group_size * head_dim)
    attn_full = jnp.dot(context, w_out, preferred_element_type=jnp.float32)
    attn_part = scatter_heads(attn_full)
    mid_rows = (tokens.astype(jnp.float32) + attn_part).astype(jnp.bfloat16)
    normed_own = rms_scale(mid_rows, ffn_gain).astype(jnp.bfloat16)
    normed_all = gather_heads(normed_own)
    shared = scatter_heads(
        jnp.dot(
            swiglu_rows(normed_all, shared_gate, shared_up),
            shared_down,
            preferred_element_type=jnp.float32,
        )
    )
    experts_total = req_total * heads_total // 2
    top_count = route_idx.shape[1]
    pair_count = tok_dev * top_count
    most_slots = 2 * max(1, (2 * pair_count + 3 * experts_total - 1) // (3 * experts_total))
    slot_total = experts_total * most_slots
    pick_list = route_idx.reshape(pair_count)
    expert_hits = (
        pick_list[:, None] == jnp.arange(experts_total, dtype=jnp.int32)[None, :]
    ).astype(jnp.int32)
    earlier = jnp.cumsum(expert_hits, axis=0) - expert_hits
    slot_index = jnp.sum(earlier * expert_hits, axis=1)
    target = (pick_list * most_slots + slot_index).reshape(tok_dev, top_count)
    slot_hit = target[:, :, None] == jnp.arange(slot_total, dtype=jnp.int32)[None, None, :]
    selector = jnp.any(slot_hit, axis=1).T.astype(jnp.bfloat16)
    slot_weight = jnp.sum(jnp.where(slot_hit, route_wt[:, :, None], 0.0), axis=1)
    half_weight = jnp.broadcast_to(
        slot_weight.reshape(tok_dev, experts_total, 1, most_slots),
        (tok_dev, experts_total, 2, most_slots),
    ).reshape(tok_dev, experts_total * 2 * most_slots)
    packed = (
        jnp.dot(selector, normed_own, preferred_element_type=jnp.float32)
        .astype(jnp.bfloat16)
        .reshape(experts_total, 1, most_slots, model_width)
    )
    outgoing = jnp.broadcast_to(packed, (experts_total, 2, most_slots, model_width)).reshape(
        experts_total * 2, most_slots, model_width
    )
    incoming = lax.all_to_all(outgoing, ("req", "head"), split_axis=0, concat_axis=0, tiled=True)
    gate_part = jnp.einsum("dsk,kf->dsf", incoming, expert_gate[0], preferred_element_type=jnp.float32)
    up_part = jnp.einsum("dsk,kf->dsf", incoming, expert_up[0], preferred_element_type=jnp.float32)
    hidden = (jax.nn.silu(gate_part) * up_part).astype(jnp.bfloat16)
    results = jnp.einsum(
        "dsf,fk->dsk", hidden, expert_down[0], preferred_element_type=jnp.float32
    ).astype(jnp.bfloat16)
    returned = lax.all_to_all(results, ("req", "head"), split_axis=0, concat_axis=0, tiled=True)
    routed = jnp.einsum(
        "tds,dsk->tk",
        half_weight.reshape(tok_dev, experts_total * 2, most_slots),
        returned.astype(jnp.float32),
        precision=lax.Precision.HIGHEST,
        preferred_element_type=jnp.float32,
    )
    result = (mid_rows.astype(jnp.float32) + shared + routed).astype(jnp.bfloat16)
    return (result, new_kv)


def solution(mesh):
    return jax.shard_map(
        per_device,
        mesh=mesh,
        in_specs=(
            P(("req", "head"), None),
            P(),
            P(None, "head"),
            P(None, "head"),
            P(None, "head"),
            P("head", None),
            P("req", "head"),
            P("req", "head"),
            P("req"),
            P(),
            P(None, "head"),
            P(None, "head"),
            P("head", None),
            P(("req", "head"), None, None),
            P(("req", "head"), None, None),
            P(("req", "head"), None, None),
            P(("req", "head"), None),
            P(("req", "head"), None),
        ),
        out_specs=(P(("req", "head"), None), P(None, "req", "head")),
        check_vma=False,
    )
```

```python
import math

import jax
import jax.numpy as jnp
from jax import lax
from jax.experimental import pallas as pl
from jax.experimental.pallas import tpu as pltpu
from jax.sharding import PartitionSpec as P

EPS = 1e-06
ROPE_BASE = 10000.0


def rms_scale(row_data, gain):
    widened = row_data.astype(jnp.float32)
    return (
        widened
        * lax.rsqrt(jnp.mean(widened * widened, axis=-1, keepdims=True) + EPS)
        * gain.astype(jnp.float32)
    )


def rotate(vectors, positions):
    half_dim = vectors.shape[-1] // 2
    steps_idx = jnp.arange(half_dim, dtype=jnp.float32)
    frequency = jnp.exp(-(2.0 * steps_idx / vectors.shape[-1]) * math.log(ROPE_BASE))
    angles = positions.astype(jnp.float32)[:, None] * frequency[None, :]
    cosine = jnp.cos(angles)[:, None, :]
    sine_part = jnp.sin(angles)[:, None, :]
    first_half = vectors[..., :half_dim]
    second_half = vectors[..., half_dim:]
    return jnp.concatenate(
        [
            first_half * cosine - second_half * sine_part,
            second_half * cosine + first_half * sine_part,
        ],
        axis=-1,
    )


def swiglu_rows(row_data, w_gate, w_up):
    gate_part = jnp.dot(row_data, w_gate, preferred_element_type=jnp.float32)
    up_part = jnp.dot(row_data, w_up, preferred_element_type=jnp.float32)
    return (jax.nn.silu(gate_part) * up_part).astype(jnp.bfloat16)


def pick_block_rows(cap_rows):
    for rows in (4864, 4096, 5120, 3840, 2432, 2560, 2048, 1920, 1280, 1024, 640, 512, 256, 128):
        if cap_rows % rows == 0:
            return rows
    return cap_rows


def cache_attention(queries, row_start, row_end, row_total, own_score, start_acc, key_cache,
                    value_cache, score_scale, tile_rows, tile_lo, tile_hi):
    q_rows, head_dim = queries.shape
    cap_rows = key_cache.shape[0]
    block_rows = pick_block_rows(cap_rows)
    grid_steps = cap_rows // block_rows
    tile_count = q_rows // tile_rows
    live_blocks = jnp.clip((row_total + block_rows - 1) // block_rows, 1, grid_steps)
    table = jnp.concatenate(
        [live_blocks.astype(jnp.int32).reshape(1), tile_lo.astype(jnp.int32),
         tile_hi.astype(jnp.int32)]
    )

    def kernel(tab_ref, q_ref, rs_ref, re_ref, m0_ref, acc0_ref, k_ref, v_ref, o_ref,
               m_sc, l_sc, acc_sc):
        step = pl.program_id(0)
        block_lo = step * block_rows

        @pl.when(step == 0)
        def _():
            m_sc[...] = m0_ref[...]
            l_sc[...] = jnp.ones_like(l_sc)
            acc_sc[...] = acc0_ref[...]

        for tile in range(tile_count):
            rows_of = pl.ds(tile * tile_rows, tile_rows)
            meets = (
                (step < tab_ref[0])
                & (tab_ref[1 + tile] < block_lo + block_rows)
                & (tab_ref[1 + tile_count + tile] > block_lo)
            )

            @pl.when(meets)
            def _():
                scores = lax.dot_general(
                    q_ref[rows_of, :], k_ref[...], (((1,), (1,)), ((), ())),
                    preferred_element_type=jnp.float32,
                ) * score_scale
                rows = block_lo + lax.broadcasted_iota(jnp.int32, (1, block_rows), 1)
                visible = (rows >= rs_ref[rows_of, :]) & (rows < re_ref[rows_of, :])
                masked = jnp.where(visible, scores, -jnp.inf)
                run_max = m_sc[rows_of, :]
                new_max = jnp.maximum(run_max, jnp.max(masked, axis=1, keepdims=True))
                weights = jnp.exp(masked - new_max)
                rescale = jnp.exp(run_max - new_max)
                l_sc[rows_of, :] = l_sc[rows_of, :] * rescale + jnp.sum(weights, axis=1, keepdims=True)
                acc_sc[rows_of, :] = acc_sc[rows_of, :] * rescale + jnp.dot(
                    weights.astype(jnp.bfloat16), v_ref[...], preferred_element_type=jnp.float32
                )
                m_sc[rows_of, :] = new_max

        @pl.when(step == pl.num_programs(0) - 1)
        def _():
            o_ref[...] = (acc_sc[...] / l_sc[...]).astype(o_ref.dtype)

    whole = lambda step, tab: (0, 0)
    cache_block = lambda step, tab: (jnp.minimum(step, tab[0] - 1), 0)
    grid_spec = pltpu.PrefetchScalarGridSpec(
        num_scalar_prefetch=1,
        grid=(grid_steps,),
        in_specs=[
            pl.BlockSpec((q_rows, head_dim), whole),
            pl.BlockSpec((q_rows, 1), whole),
            pl.BlockSpec((q_rows, 1), whole),
            pl.BlockSpec((q_rows, 1), whole),
            pl.BlockSpec((q_rows, head_dim), whole),
            pl.BlockSpec((block_rows, head_dim), cache_block),
            pl.BlockSpec((block_rows, head_dim), cache_block),
        ],
        out_specs=pl.BlockSpec((q_rows, head_dim), whole),
        scratch_shapes=[
            pltpu.VMEM((q_rows, 1), jnp.float32),
            pltpu.VMEM((q_rows, 1), jnp.float32),
            pltpu.VMEM((q_rows, head_dim), jnp.float32),
        ],
    )
    return pl.pallas_call(
        kernel,
        grid_spec=grid_spec,
        out_shape=jax.ShapeDtypeStruct((q_rows, head_dim), jnp.bfloat16),
        compiler_params=pltpu.CompilerParams(dimension_semantics=("arbitrary",)),
    )(table, queries, row_start, row_end, own_score, start_acc, key_cache, value_cache)


def head_shift(values, shift):
    heads = lax.axis_size("head")
    return lax.ppermute(values, "head", [(j, (j + shift) % heads) for j in range(heads)])


def gather_heads(values):
    heads = lax.axis_size("head")
    return jnp.concatenate([values] + [head_shift(values, -s) for s in range(1, heads)], axis=0)


def scatter_heads(values):
    heads = lax.axis_size("head")
    parts = values.reshape(heads, values.shape[0] // heads, *values.shape[1:])
    total = parts[0]
    for s in range(1, heads):
        total = total + head_shift(parts[s], s)
    return total


def to_rotated(values, chunk):
    heads = lax.axis_size("head")
    offset = lax.axis_index("head") * chunk
    doubled = jnp.concatenate([values, values], axis=0)
    return lax.dynamic_slice_in_dim(doubled, offset, heads * chunk, 0)


def from_rotated(values, chunk):
    heads = lax.axis_size("head")
    offset = (heads - lax.axis_index("head")) % heads * chunk
    doubled = jnp.concatenate([values, values], axis=0)
    return lax.dynamic_slice_in_dim(doubled, offset, heads * chunk, 0)


def per_device(
    tokens,
    attn_gain,
    w_query,
    w_key,
    w_value,
    w_out,
    key_cache,
    value_cache,
    lengths,
    ffn_gain,
    shared_gate,
    shared_up,
    shared_down,
    expert_gate,
    expert_up,
    expert_down,
    route_idx,
    route_wt,
):
    tok_dev, model_width = tokens.shape
    heads_total = lax.axis_size("head")
    req_total = lax.axis_size("req")
    all_tok = gather_heads(tokens)
    req_dev = all_tok.shape[0]
    head_dim = w_key.shape[1]
    group_size = w_query.shape[1] // head_dim
    starts = jnp.cumsum(lengths) - lengths
    row_total = jnp.sum(lengths)
    lengths_rot = to_rotated(lengths, tok_dev)
    starts_rot = to_rotated(starts, tok_dev)
    normed = rms_scale(all_tok, attn_gain).astype(jnp.bfloat16)
    queries = rotate(
        jnp.dot(normed, w_query, preferred_element_type=jnp.float32).reshape(
            req_dev, group_size, head_dim
        ),
        lengths_rot,
    ).astype(jnp.bfloat16)
    new_key = rotate(
        jnp.dot(normed, w_key, preferred_element_type=jnp.float32)[:, None, :], lengths_rot
    )[:, 0, :].astype(jnp.bfloat16)
    new_value = jnp.dot(normed, w_value, preferred_element_type=jnp.float32).astype(jnp.bfloat16)
    new_kv = from_rotated(jnp.stack([new_key, new_value], axis=1), tok_dev).transpose(1, 0, 2)
    score_scale = 1.0 / math.sqrt(head_dim)
    flat_queries = queries.reshape(req_dev * group_size, head_dim)
    own_score = (
        jnp.einsum("rgd,rd->rg", queries, new_key, preferred_element_type=jnp.float32).reshape(-1, 1)
        * score_scale
    )
    row_start = jnp.repeat(starts_rot, group_size)[:, None]
    row_end = jnp.repeat(starts_rot + lengths_rot, group_size)[:, None]
    start_acc = jnp.repeat(new_value, group_size, axis=0).astype(jnp.float32)
    tile_reqs = 16 if req_dev % 16 == 0 else req_dev
    ends_rot = starts_rot + lengths_rot
    context = cache_attention(
        flat_queries, row_start, row_end, row_total, own_score, start_acc, key_cache, value_cache,
        score_scale, tile_reqs * group_size,
        jnp.min(starts_rot.reshape(-1, tile_reqs), axis=1),
        jnp.max(ends_rot.reshape(-1, tile_reqs), axis=1),
    ).reshape(req_dev, group_size * head_dim)
    attn_part = scatter_heads(jnp.dot(context, w_out, preferred_element_type=jnp.float32))
    mid_rows = (tokens.astype(jnp.float32) + attn_part).astype(jnp.bfloat16)
    normed_own = rms_scale(mid_rows, ffn_gain).astype(jnp.bfloat16)
    normed_all = gather_heads(normed_own)
    shared = scatter_heads(
        jnp.dot(
            swiglu_rows(normed_all, shared_gate, shared_up),
            shared_down,
            preferred_element_type=jnp.float32,
        )
    )
    experts_total = req_total * heads_total // 2
    top_count = route_idx.shape[1]
    pair_count = tok_dev * top_count
    most_slots = 2 * max(1, (2 * pair_count + 3 * experts_total - 1) // (3 * experts_total))
    slot_total = experts_total * most_slots
    pick_list = route_idx.reshape(pair_count)
    expert_hits = (
        pick_list[:, None] == jnp.arange(experts_total, dtype=jnp.int32)[None, :]
    ).astype(jnp.int32)
    earlier = jnp.cumsum(expert_hits, axis=0) - expert_hits
    slot_index = jnp.sum(earlier * expert_hits, axis=1)
    target = (pick_list * most_slots + slot_index).reshape(tok_dev, top_count)
    slot_hit = target[:, :, None] == jnp.arange(slot_total, dtype=jnp.int32)[None, None, :]
    selector = jnp.any(slot_hit, axis=1).T.astype(jnp.bfloat16)
    packed = (
        jnp.dot(selector, normed_own, preferred_element_type=jnp.float32)
        .astype(jnp.bfloat16)
        .reshape(experts_total, 1, most_slots, model_width)
    )
    outgoing = jnp.broadcast_to(packed, (experts_total, 2, most_slots, model_width)).reshape(
        experts_total * 2 * most_slots, model_width
    )
    incoming = lax.all_to_all(outgoing, ("req", "head"), split_axis=0, concat_axis=0, tiled=True)
    hidden = swiglu_rows(incoming, expert_gate[0], expert_up[0])
    results = jnp.dot(hidden, expert_down[0], preferred_element_type=jnp.float32).astype(
        jnp.bfloat16
    )
    returned = lax.all_to_all(results, ("req", "head"), split_axis=0, concat_axis=0, tiled=True)
    slot_weight = jnp.sum(jnp.where(slot_hit, route_wt[:, :, None], 0.0), axis=1)
    half_weight = jnp.broadcast_to(
        slot_weight.reshape(tok_dev, experts_total, 1, most_slots),
        (tok_dev, experts_total, 2, most_slots),
    ).reshape(tok_dev, experts_total * 2 * most_slots)
    routed = jnp.dot(
        half_weight,
        returned.astype(jnp.float32),
        precision=lax.Precision.HIGHEST,
        preferred_element_type=jnp.float32,
    )
    result = (mid_rows.astype(jnp.float32) + shared + routed).astype(jnp.bfloat16)
    return (result, new_kv)


def solution(mesh):
    return jax.shard_map(
        per_device,
        mesh=mesh,
        in_specs=(
            P(("req", "head"), None),
            P(),
            P(None, "head"),
            P(None, "head"),
            P(None, "head"),
            P("head", None),
            P("req", "head"),
            P("req", "head"),
            P("req"),
            P(),
            P(None, "head"),
            P(None, "head"),
            P("head", None),
            P(("req", "head"), None, None),
            P(("req", "head"), None, None),
            P(("req", "head"), None, None),
            P(("req", "head"), None),
            P(("req", "head"), None),
        ),
        out_specs=(P(("req", "head"), None), P(None, "req", "head")),
        check_vma=False,
    )
```

```python
import math

import jax
import jax.numpy as jnp
from jax import lax
from jax.experimental import pallas as pl
from jax.experimental.pallas import tpu as pltpu
from jax.sharding import PartitionSpec as P

EPS = 1e-06
ROPE_BASE = 10000.0


def rms_scale(row_data, gain):
    widened = row_data.astype(jnp.float32)
    return (
        widened
        * lax.rsqrt(jnp.mean(widened * widened, axis=-1, keepdims=True) + EPS)
        * gain.astype(jnp.float32)
    )


def rotate(vectors, positions):
    half_dim = vectors.shape[-1] // 2
    steps_idx = jnp.arange(half_dim, dtype=jnp.float32)
    frequency = jnp.exp(-(2.0 * steps_idx / vectors.shape[-1]) * math.log(ROPE_BASE))
    angles = positions.astype(jnp.float32)[:, None] * frequency[None, :]
    cosine = jnp.cos(angles)[:, None, :]
    sine_part = jnp.sin(angles)[:, None, :]
    first_half = vectors[..., :half_dim]
    second_half = vectors[..., half_dim:]
    return jnp.concatenate(
        [
            first_half * cosine - second_half * sine_part,
            second_half * cosine + first_half * sine_part,
        ],
        axis=-1,
    )


def swiglu_rows(row_data, w_gate, w_up):
    gate_part = jnp.dot(row_data, w_gate, preferred_element_type=jnp.float32)
    up_part = jnp.dot(row_data, w_up, preferred_element_type=jnp.float32)
    return (jax.nn.silu(gate_part) * up_part).astype(jnp.bfloat16)


def pick_block_rows(cap_rows):
    for rows in (4864, 4096, 5120, 3840, 2432, 2560, 2048, 1920, 1280, 1024, 640, 512, 256, 128):
        if cap_rows % rows == 0:
            return rows
    return cap_rows


def cache_attention(queries, row_start, row_end, row_total, fresh_key, fresh_value, key_cache,
                    value_cache, score_scale, tile_rows, tile_lo, tile_hi):
    q_rows, head_dim = queries.shape
    fresh_rows = fresh_key.shape[0]
    group_size = q_rows // fresh_rows
    cap_rows = key_cache.shape[0]
    block_rows = pick_block_rows(cap_rows)
    grid_steps = cap_rows // block_rows
    tile_count = q_rows // tile_rows
    live_blocks = jnp.clip((row_total + block_rows - 1) // block_rows, 1, grid_steps)
    table = jnp.concatenate(
        [live_blocks.astype(jnp.int32).reshape(1), tile_lo.astype(jnp.int32),
         tile_hi.astype(jnp.int32)]
    )

    def kernel(tab_ref, q_ref, rs_ref, re_ref, kn_ref, vn_ref, k_ref, v_ref, o_ref,
               m_sc, l_sc, acc_sc):
        step = pl.program_id(0)
        block_lo = step * block_rows

        @pl.when(step == 0)
        def _():
            owner = lax.broadcasted_iota(jnp.int32, (q_rows, fresh_rows), 0) // group_size
            column = lax.broadcasted_iota(jnp.int32, (q_rows, fresh_rows), 1)
            expand = (owner == column).astype(jnp.bfloat16)
            key_rows = jnp.dot(expand, kn_ref[...], preferred_element_type=jnp.float32)
            m_sc[...] = (
                jnp.sum(q_ref[...].astype(jnp.float32) * key_rows, axis=1, keepdims=True)
                * score_scale
            )
            l_sc[...] = jnp.ones_like(l_sc)
            acc_sc[...] = jnp.dot(expand, vn_ref[...], preferred_element_type=jnp.float32)

        for tile in range(tile_count):
            rows_of = pl.ds(tile * tile_rows, tile_rows)
            meets = (
                (step < tab_ref[0])
                & (tab_ref[1 + tile] < block_lo + block_rows)
                & (tab_ref[1 + tile_count + tile] > block_lo)
            )

            @pl.when(meets)
            def _():
                scores = lax.dot_general(
                    q_ref[rows_of, :], k_ref[...], (((1,), (1,)), ((), ())),
                    preferred_element_type=jnp.float32,
                ) * score_scale
                rows = block_lo + lax.broadcasted_iota(jnp.int32, (1, block_rows), 1)
                visible = (rows >= rs_ref[rows_of, :]) & (rows < re_ref[rows_of, :])
                masked = jnp.where(visible, scores, -jnp.inf)
                run_max = m_sc[rows_of, :]
                new_max = jnp.maximum(run_max, jnp.max(masked, axis=1, keepdims=True))
                weights = jnp.exp(masked - new_max)
                rescale = jnp.exp(run_max - new_max)
                l_sc[rows_of, :] = l_sc[rows_of, :] * rescale + jnp.sum(weights, axis=1, keepdims=True)
                acc_sc[rows_of, :] = acc_sc[rows_of, :] * rescale + jnp.dot(
                    weights.astype(jnp.bfloat16), v_ref[...], preferred_element_type=jnp.float32
                )
                m_sc[rows_of, :] = new_max

        @pl.when(step == pl.num_programs(0) - 1)
        def _():
            o_ref[...] = (acc_sc[...] / l_sc[...]).astype(o_ref.dtype)

    whole = lambda step, tab: (0, 0)
    cache_block = lambda step, tab: (jnp.minimum(step, tab[0] - 1), 0)
    grid_spec = pltpu.PrefetchScalarGridSpec(
        num_scalar_prefetch=1,
        grid=(grid_steps,),
        in_specs=[
            pl.BlockSpec((q_rows, head_dim), whole),
            pl.BlockSpec((q_rows, 1), whole),
            pl.BlockSpec((q_rows, 1), whole),
            pl.BlockSpec((fresh_rows, head_dim), whole),
            pl.BlockSpec((fresh_rows, head_dim), whole),
            pl.BlockSpec((block_rows, head_dim), cache_block),
            pl.BlockSpec((block_rows, head_dim), cache_block),
        ],
        out_specs=pl.BlockSpec((q_rows, head_dim), whole),
        scratch_shapes=[
            pltpu.VMEM((q_rows, 1), jnp.float32),
            pltpu.VMEM((q_rows, 1), jnp.float32),
            pltpu.VMEM((q_rows, head_dim), jnp.float32),
        ],
    )
    return pl.pallas_call(
        kernel,
        grid_spec=grid_spec,
        out_shape=jax.ShapeDtypeStruct((q_rows, head_dim), jnp.bfloat16),
        compiler_params=pltpu.CompilerParams(dimension_semantics=("arbitrary",)),
    )(table, queries, row_start, row_end, fresh_key, fresh_value, key_cache, value_cache)


def head_shift(values, shift):
    heads = lax.axis_size("head")
    return lax.ppermute(values, "head", [(j, (j + shift) % heads) for j in range(heads)])


def gather_heads(values):
    heads = lax.axis_size("head")
    return jnp.concatenate([values] + [head_shift(values, -s) for s in range(1, heads)], axis=0)


def scatter_heads(values):
    heads = lax.axis_size("head")
    parts = values.reshape(heads, values.shape[0] // heads, *values.shape[1:])
    total = parts[0]
    for s in range(1, heads):
        total = total + head_shift(parts[s], s)
    return total


def to_rotated(values, chunk):
    heads = lax.axis_size("head")
    offset = lax.axis_index("head") * chunk
    doubled = jnp.concatenate([values, values], axis=0)
    return lax.dynamic_slice_in_dim(doubled, offset, heads * chunk, 0)


def from_rotated(values, chunk):
    heads = lax.axis_size("head")
    offset = (heads - lax.axis_index("head")) % heads * chunk
    doubled = jnp.concatenate([values, values], axis=0)
    return lax.dynamic_slice_in_dim(doubled, offset, heads * chunk, 0)


def per_device(
    tokens,
    attn_gain,
    w_query,
    w_key,
    w_value,
    w_out,
    key_cache,
    value_cache,
    lengths,
    ffn_gain,
    shared_gate,
    shared_up,
    shared_down,
    expert_gate,
    expert_up,
    expert_down,
    route_idx,
    route_wt,
):
    tok_dev, model_width = tokens.shape
    heads_total = lax.axis_size("head")
    req_total = lax.axis_size("req")
    all_tok = gather_heads(tokens)
    req_dev = all_tok.shape[0]
    head_dim = w_key.shape[1]
    group_size = w_query.shape[1] // head_dim
    starts = jnp.cumsum(lengths) - lengths
    row_total = jnp.sum(lengths)
    lengths_rot = to_rotated(lengths, tok_dev)
    starts_rot = to_rotated(starts, tok_dev)
    normed = rms_scale(all_tok, attn_gain).astype(jnp.bfloat16)
    queries = rotate(
        jnp.dot(normed, w_query, preferred_element_type=jnp.float32).reshape(
            req_dev, group_size, head_dim
        ),
        lengths_rot,
    ).astype(jnp.bfloat16)
    new_key = rotate(
        jnp.dot(normed, w_key, preferred_element_type=jnp.float32)[:, None, :], lengths_rot
    )[:, 0, :].astype(jnp.bfloat16)
    new_value = jnp.dot(normed, w_value, preferred_element_type=jnp.float32).astype(jnp.bfloat16)
    new_kv = from_rotated(jnp.stack([new_key, new_value], axis=1), tok_dev).transpose(1, 0, 2)
    score_scale = 1.0 / math.sqrt(head_dim)
    flat_queries = queries.reshape(req_dev * group_size, head_dim)
    row_start = jnp.repeat(starts_rot, group_size)[:, None]
    row_end = jnp.repeat(starts_rot + lengths_rot, group_size)[:, None]
    tile_reqs = 16 if req_dev % 16 == 0 else req_dev
    ends_rot = starts_rot + lengths_rot
    context = cache_attention(
        flat_queries, row_start, row_end, row_total, new_key, new_value, key_cache, value_cache,
        score_scale, tile_reqs * group_size,
        jnp.min(starts_rot.reshape(-1, tile_reqs), axis=1),
        jnp.max(ends_rot.reshape(-1, tile_reqs), axis=1),
    ).reshape(req_dev, group_size * head_dim)
    attn_part = scatter_heads(jnp.dot(context, w_out, preferred_element_type=jnp.float32))
    mid_rows = (tokens.astype(jnp.float32) + attn_part).astype(jnp.bfloat16)
    normed_own = rms_scale(mid_rows, ffn_gain).astype(jnp.bfloat16)
    normed_all = gather_heads(normed_own)
    shared = scatter_heads(
        jnp.dot(
            swiglu_rows(normed_all, shared_gate, shared_up),
            shared_down,
            preferred_element_type=jnp.float32,
        )
    )
    experts_total = req_total * heads_total // 2
    top_count = route_idx.shape[1]
    pair_count = tok_dev * top_count
    most_slots = 2 * max(1, (2 * pair_count + 3 * experts_total - 1) // (3 * experts_total))
    slot_total = experts_total * most_slots
    pick_list = route_idx.reshape(pair_count)
    expert_hits = (
        pick_list[:, None] == jnp.arange(experts_total, dtype=jnp.int32)[None, :]
    ).astype(jnp.int32)
    earlier = jnp.cumsum(expert_hits, axis=0) - expert_hits
    slot_index = jnp.sum(earlier * expert_hits, axis=1)
    target = (pick_list * most_slots + slot_index).reshape(tok_dev, top_count)
    slot_hit = target[:, :, None] == jnp.arange(slot_total, dtype=jnp.int32)[None, None, :]
    selector = jnp.any(slot_hit, axis=1).T.astype(jnp.bfloat16)
    packed = (
        jnp.dot(selector, normed_own, preferred_element_type=jnp.float32)
        .astype(jnp.bfloat16)
        .reshape(experts_total, 1, most_slots, model_width)
    )
    outgoing = jnp.broadcast_to(packed, (experts_total, 2, most_slots, model_width)).reshape(
        experts_total * 2 * most_slots, model_width
    )
    incoming = lax.all_to_all(outgoing, ("req", "head"), split_axis=0, concat_axis=0, tiled=True)
    hidden = swiglu_rows(incoming, expert_gate[0], expert_up[0])
    results = jnp.dot(hidden, expert_down[0], preferred_element_type=jnp.float32).astype(
        jnp.bfloat16
    )
    returned = lax.all_to_all(results, ("req", "head"), split_axis=0, concat_axis=0, tiled=True)
    slot_weight = jnp.sum(jnp.where(slot_hit, route_wt[:, :, None], 0.0), axis=1)
    half_weight = jnp.broadcast_to(
        slot_weight.reshape(tok_dev, experts_total, 1, most_slots),
        (tok_dev, experts_total, 2, most_slots),
    ).reshape(tok_dev, experts_total * 2 * most_slots)
    routed = jnp.dot(
        half_weight,
        returned.astype(jnp.float32),
        precision=lax.Precision.HIGHEST,
        preferred_element_type=jnp.float32,
    )
    result = (mid_rows.astype(jnp.float32) + shared + routed).astype(jnp.bfloat16)
    return (result, new_kv)


def solution(mesh):
    return jax.shard_map(
        per_device,
        mesh=mesh,
        in_specs=(
            P(("req", "head"), None),
            P(),
            P(None, "head"),
            P(None, "head"),
            P(None, "head"),
            P("head", None),
            P("req", "head"),
            P("req", "head"),
            P("req"),
            P(),
            P(None, "head"),
            P(None, "head"),
            P("head", None),
            P(("req", "head"), None, None),
            P(("req", "head"), None, None),
            P(("req", "head"), None, None),
            P(("req", "head"), None),
            P(("req", "head"), None),
        ),
        out_specs=(P(("req", "head"), None), P(None, "req", "head")),
        check_vma=False,
    )
```

```python
import math

import jax
import jax.numpy as jnp
from jax import lax
from jax.experimental import pallas as pl
from jax.experimental.pallas import tpu as pltpu
from jax.sharding import PartitionSpec as P

EPS = 1e-06
ROPE_BASE = 10000.0


def rms_scale(row_data, gain):
    widened = row_data.astype(jnp.float32)
    return (
        widened
        * lax.rsqrt(jnp.mean(widened * widened, axis=-1, keepdims=True) + EPS)
        * gain.astype(jnp.float32)
    )


def rotate(vectors, positions):
    half_dim = vectors.shape[-1] // 2
    steps_idx = jnp.arange(half_dim, dtype=jnp.float32)
    frequency = jnp.exp(-(2.0 * steps_idx / vectors.shape[-1]) * math.log(ROPE_BASE))
    angles = positions.astype(jnp.float32)[:, None] * frequency[None, :]
    cosine = jnp.cos(angles)[:, None, :]
    sine_part = jnp.sin(angles)[:, None, :]
    first_half = vectors[..., :half_dim]
    second_half = vectors[..., half_dim:]
    return jnp.concatenate(
        [
            first_half * cosine - second_half * sine_part,
            second_half * cosine + first_half * sine_part,
        ],
        axis=-1,
    )


def swiglu_rows(row_data, w_gate, w_up):
    gate_part = jnp.dot(row_data, w_gate, preferred_element_type=jnp.float32)
    up_part = jnp.dot(row_data, w_up, preferred_element_type=jnp.float32)
    return (jax.nn.silu(gate_part) * up_part).astype(jnp.bfloat16)


def pick_block_rows(cap_rows):
    for rows in (4864, 4096, 5120, 3840, 2432, 2560, 2048, 1920, 1280, 1024, 640, 512, 256, 128):
        if cap_rows % rows == 0:
            return rows
    return cap_rows


def cache_attention(queries, row_bounds, row_total, fresh_key, fresh_value, key_cache,
                    value_cache, score_scale, tile_rows, tile_lo, tile_hi):
    q_rows, head_dim = queries.shape
    fresh_rows = fresh_key.shape[0]
    group_size = q_rows // fresh_rows
    cap_rows = key_cache.shape[0]
    block_rows = pick_block_rows(cap_rows)
    grid_steps = cap_rows // block_rows
    tile_count = q_rows // tile_rows
    live_blocks = jnp.clip((row_total + block_rows - 1) // block_rows, 1, grid_steps)
    table = jnp.concatenate(
        [live_blocks.astype(jnp.int32).reshape(1), tile_lo.astype(jnp.int32),
         tile_hi.astype(jnp.int32)]
    )

    def kernel(tab_ref, q_ref, b_ref, kn_ref, vn_ref, k_ref, v_ref, o_ref,
               m_sc, l_sc, acc_sc):
        step = pl.program_id(0)
        block_lo = step * block_rows

        @pl.when(step == 0)
        def _():
            owner = lax.broadcasted_iota(jnp.int32, (q_rows, fresh_rows), 0) // group_size
            column = lax.broadcasted_iota(jnp.int32, (q_rows, fresh_rows), 1)
            expand = (owner == column).astype(jnp.bfloat16)
            key_rows = jnp.dot(expand, kn_ref[...], preferred_element_type=jnp.float32)
            m_sc[...] = (
                jnp.sum(q_ref[...].astype(jnp.float32) * key_rows, axis=1, keepdims=True)
                * score_scale
            )
            l_sc[...] = jnp.ones_like(l_sc)
            acc_sc[...] = jnp.dot(expand, vn_ref[...], preferred_element_type=jnp.float32)

        for tile in range(tile_count):
            rows_of = pl.ds(tile * tile_rows, tile_rows)
            meets = (
                (step < tab_ref[0])
                & (tab_ref[1 + tile] < block_lo + block_rows)
                & (tab_ref[1 + tile_count + tile] > block_lo)
            )

            @pl.when(meets)
            def _():
                scores = lax.dot_general(
                    q_ref[rows_of, :], k_ref[...], (((1,), (1,)), ((), ())),
                    preferred_element_type=jnp.float32,
                ) * score_scale
                rows = block_lo + lax.broadcasted_iota(jnp.int32, (1, block_rows), 1)
                visible = (rows >= b_ref[rows_of, 0:1]) & (rows < b_ref[rows_of, 1:2])
                masked = jnp.where(visible, scores, -jnp.inf)
                run_max = m_sc[rows_of, :]
                new_max = jnp.maximum(run_max, jnp.max(masked, axis=1, keepdims=True))
                weights = jnp.exp(masked - new_max)
                rescale = jnp.exp(run_max - new_max)
                l_sc[rows_of, :] = l_sc[rows_of, :] * rescale + jnp.sum(weights, axis=1, keepdims=True)
                acc_sc[rows_of, :] = acc_sc[rows_of, :] * rescale + jnp.dot(
                    weights.astype(jnp.bfloat16), v_ref[...], preferred_element_type=jnp.float32
                )
                m_sc[rows_of, :] = new_max

        @pl.when(step == pl.num_programs(0) - 1)
        def _():
            o_ref[...] = (acc_sc[...] / l_sc[...]).astype(o_ref.dtype)

    whole = lambda step, tab: (0, 0)
    cache_block = lambda step, tab: (jnp.minimum(step, tab[0] - 1), 0)
    grid_spec = pltpu.PrefetchScalarGridSpec(
        num_scalar_prefetch=1,
        grid=(grid_steps,),
        in_specs=[
            pl.BlockSpec((q_rows, head_dim), whole),
            pl.BlockSpec((q_rows, 2), whole),
            pl.BlockSpec((fresh_rows, head_dim), whole),
            pl.BlockSpec((fresh_rows, head_dim), whole),
            pl.BlockSpec((block_rows, head_dim), cache_block),
            pl.BlockSpec((block_rows, head_dim), cache_block),
        ],
        out_specs=pl.BlockSpec((q_rows, head_dim), whole),
        scratch_shapes=[
            pltpu.VMEM((q_rows, 1), jnp.float32),
            pltpu.VMEM((q_rows, 1), jnp.float32),
            pltpu.VMEM((q_rows, head_dim), jnp.float32),
        ],
    )
    return pl.pallas_call(
        kernel,
        grid_spec=grid_spec,
        out_shape=jax.ShapeDtypeStruct((q_rows, head_dim), jnp.bfloat16),
        compiler_params=pltpu.CompilerParams(dimension_semantics=("arbitrary",)),
    )(table, queries, row_bounds, fresh_key, fresh_value, key_cache, value_cache)


def head_shift(values, shift):
    heads = lax.axis_size("head")
    return lax.ppermute(values, "head", [(j, (j + shift) % heads) for j in range(heads)])


def gather_heads(values):
    heads = lax.axis_size("head")
    return jnp.concatenate([values] + [head_shift(values, -s) for s in range(1, heads)], axis=0)


def scatter_heads(values):
    heads = lax.axis_size("head")
    parts = values.reshape(heads, values.shape[0] // heads, *values.shape[1:])
    total = parts[0]
    for s in range(1, heads):
        total = total + head_shift(parts[s], s)
    return total


def to_rotated(values, chunk):
    heads = lax.axis_size("head")
    offset = lax.axis_index("head") * chunk
    doubled = jnp.concatenate([values, values], axis=0)
    return lax.dynamic_slice_in_dim(doubled, offset, heads * chunk, 0)


def from_rotated(values, chunk):
    heads = lax.axis_size("head")
    offset = (heads - lax.axis_index("head")) % heads * chunk
    doubled = jnp.concatenate([values, values], axis=0)
    return lax.dynamic_slice_in_dim(doubled, offset, heads * chunk, 0)


def per_device(
    tokens,
    attn_gain,
    w_query,
    w_key,
    w_value,
    w_out,
    key_cache,
    value_cache,
    lengths,
    ffn_gain,
    shared_gate,
    shared_up,
    shared_down,
    expert_gate,
    expert_up,
    expert_down,
    route_idx,
    route_wt,
):
    tok_dev, model_width = tokens.shape
    heads_total = lax.axis_size("head")
    req_total = lax.axis_size("req")
    all_tok = gather_heads(tokens)
    req_dev = all_tok.shape[0]
    head_dim = w_key.shape[1]
    group_size = w_query.shape[1] // head_dim
    starts = jnp.cumsum(lengths) - lengths
    row_total = jnp.sum(lengths)
    lengths_rot = to_rotated(lengths, tok_dev)
    starts_rot = to_rotated(starts, tok_dev)
    normed = rms_scale(all_tok, attn_gain).astype(jnp.bfloat16)
    queries = rotate(
        jnp.dot(normed, w_query, preferred_element_type=jnp.float32).reshape(
            req_dev, group_size, head_dim
        ),
        lengths_rot,
    ).astype(jnp.bfloat16)
    new_key = rotate(
        jnp.dot(normed, w_key, preferred_element_type=jnp.float32)[:, None, :], lengths_rot
    )[:, 0, :].astype(jnp.bfloat16)
    new_value = jnp.dot(normed, w_value, preferred_element_type=jnp.float32).astype(jnp.bfloat16)
    new_kv = from_rotated(jnp.stack([new_key, new_value], axis=1), tok_dev).transpose(1, 0, 2)
    score_scale = 1.0 / math.sqrt(head_dim)
    flat_queries = queries.reshape(req_dev * group_size, head_dim)
    row_bounds = jnp.repeat(
        jnp.stack([starts_rot, starts_rot + lengths_rot], axis=1), group_size, axis=0
    )
    tile_reqs = 16 if req_dev % 16 == 0 else req_dev
    ends_rot = starts_rot + lengths_rot
    context = cache_attention(
        flat_queries, row_bounds, row_total, new_key, new_value, key_cache, value_cache,
        score_scale, tile_reqs * group_size,
        jnp.min(starts_rot.reshape(-1, tile_reqs), axis=1),
        jnp.max(ends_rot.reshape(-1, tile_reqs), axis=1),
    ).reshape(req_dev, group_size * head_dim)
    attn_part = scatter_heads(jnp.dot(context, w_out, preferred_element_type=jnp.float32))
    mid_rows = (tokens.astype(jnp.float32) + attn_part).astype(jnp.bfloat16)
    normed_own = rms_scale(mid_rows, ffn_gain).astype(jnp.bfloat16)
    normed_all = gather_heads(normed_own)
    shared = scatter_heads(
        jnp.dot(
            swiglu_rows(normed_all, shared_gate, shared_up),
            shared_down,
            preferred_element_type=jnp.float32,
        )
    )
    experts_total = req_total * heads_total // 2
    top_count = route_idx.shape[1]
    pair_count = tok_dev * top_count
    most_slots = 2 * max(1, (2 * pair_count + 3 * experts_total - 1) // (3 * experts_total))
    slot_total = experts_total * most_slots
    pick_list = route_idx.reshape(pair_count)
    expert_hits = (
        pick_list[:, None] == jnp.arange(experts_total, dtype=jnp.int32)[None, :]
    ).astype(jnp.int32)
    earlier = jnp.cumsum(expert_hits, axis=0) - expert_hits
    slot_index = jnp.sum(earlier * expert_hits, axis=1)
    target = (pick_list * most_slots + slot_index).reshape(tok_dev, top_count)
    slot_hit = target[:, :, None] == jnp.arange(slot_total, dtype=jnp.int32)[None, None, :]
    selector = jnp.any(slot_hit, axis=1).T.astype(jnp.bfloat16)
    packed = (
        jnp.dot(selector, normed_own, preferred_element_type=jnp.float32)
        .astype(jnp.bfloat16)
        .reshape(experts_total, 1, most_slots, model_width)
    )
    outgoing = jnp.broadcast_to(packed, (experts_total, 2, most_slots, model_width)).reshape(
        experts_total * 2 * most_slots, model_width
    )
    incoming = lax.all_to_all(outgoing, ("req", "head"), split_axis=0, concat_axis=0, tiled=True)
    hidden = swiglu_rows(incoming, expert_gate[0], expert_up[0])
    results = jnp.dot(hidden, expert_down[0], preferred_element_type=jnp.float32).astype(
        jnp.bfloat16
    )
    returned = lax.all_to_all(results, ("req", "head"), split_axis=0, concat_axis=0, tiled=True)
    slot_weight = jnp.sum(jnp.where(slot_hit, route_wt[:, :, None], 0.0), axis=1)
    half_weight = jnp.broadcast_to(
        slot_weight.reshape(tok_dev, experts_total, 1, most_slots),
        (tok_dev, experts_total, 2, most_slots),
    ).reshape(tok_dev, experts_total * 2 * most_slots)
    routed = jnp.dot(
        half_weight,
        returned.astype(jnp.float32),
        precision=lax.Precision.HIGHEST,
        preferred_element_type=jnp.float32,
    )
    result = (mid_rows.astype(jnp.float32) + shared + routed).astype(jnp.bfloat16)
    return (result, new_kv)


def solution(mesh):
    return jax.shard_map(
        per_device,
        mesh=mesh,
        in_specs=(
            P(("req", "head"), None),
            P(),
            P(None, "head"),
            P(None, "head"),
            P(None, "head"),
            P("head", None),
            P("req", "head"),
            P("req", "head"),
            P("req"),
            P(),
            P(None, "head"),
            P(None, "head"),
            P("head", None),
            P(("req", "head"), None, None),
            P(("req", "head"), None, None),
            P(("req", "head"), None, None),
            P(("req", "head"), None),
            P(("req", "head"), None),
        ),
        out_specs=(P(("req", "head"), None), P(None, "req", "head")),
        check_vma=False,
    )
```
